512 devices in a mesh: seq: 128 (over z, y_hi, x, core), head: 4 (over y_lo).
Axes of the slice: x: 4, y: 8 (y_hi: 2, y_lo: 4; y = y_hi * 4 + y_lo), z: 8, core: 2. Of those that a mesh axis runs over, the one named last changes fastest.
Arguments:
- query_rows: bfloat16 [32768, 8, 128], P('seq', 'head'), may hold values from -20 to 20
- key_rows: bfloat16 [32768, 8, 128], P('seq', 'head'), may hold values from -20 to 20
- value_rows: bfloat16 [32768, 8, 128], P('seq', 'head'), may hold values from -6 to 6
- cotangent: bfloat16 [32768, 8, 128], P('seq', 'head'), may hold values from -6 to 6
- norm_gain: float32 [8, 128], P('head'), may hold values from 0.5 to 2
- offsets: int32 [8], P('head'), may hold values from 0 to 31, as said below
Outputs:
- query_grad: bfloat16 [32768, 8, 128], P('seq', 'head')
- key_grad: bfloat16 [32768, 8, 128], P('seq', 'head')
- value_grad: bfloat16 [32768, 8, 128], P('seq', 'head')
The draws below stay inside these ranges and needn't reach their ends.
Inputs may be any that keep to these rules, and one draw needn't show every extreme that they name: The heads' offsets are distinct.
All inputs are finite; a program needn't handle non-finite values.
Results may differ from the reference program's by a relative error of at most 0.018.
Values may be sent and summed in bfloat16 or wider, within the bound.
No kernel may reach another device: no remote copies, remote signals or barrier semaphores. Data moves between devices by JAX's collectives and lax.ppermute only.
A program may use at most 128 MiB of HBM per device.

```python
import math
import jax
import jax.numpy as jnp
from jax import lax

HD = 128
HEADS = 8
RATE2 = 4
RATE3 = 16
RATE4 = 32
TOKENS = 32768
SEL = 1024


def paired_rows(key):
    full_shape = (TOKENS, HEADS, HD)
    queries = jnp.clip(jax.random.normal(jax.random.fold_in(key, 11), full_shape, jnp.float32), -6.0, 6.0)
    keyed = jnp.clip(jax.random.normal(jax.random.fold_in(key, 12), full_shape, jnp.float32), -6.0, 6.0)
    return (queries, keyed)


def draw_query_rows(key, part):
    return paired_rows(key)[0].astype(jnp.bfloat16)


def draw_key_rows(key, part):
    return paired_rows(key)[1].astype(jnp.bfloat16)


def draw_offsets(key, part):
    inner = jax.random.permutation(jax.random.fold_in(key, 21), 30).astype(jnp.int32) + 1
    chosen = jnp.concatenate([jnp.array([0, 31], dtype=jnp.int32), inner[:HEADS - 2]])
    return jax.random.permutation(jax.random.fold_in(key, 22), chosen).astype(jnp.int32)


def level_of(rng, extent, shards, least, largest):
    def one(axis_at, shards_of):
        draws = jax.random.uniform(jax.random.fold_in(jax.random.fold_in(rng, 6), axis_at), (shards_of,), jnp.float32, least / len(shards), largest / len(shards))
        return jnp.repeat(jnp.exp(draws), extent[axis_at] // shards_of).reshape((-1,) + (1,) * (len(extent) - axis_at - 1))

    factor_of = one(*shards[0])
    for cut in shards[1:]:
        factor_of = factor_of * one(*cut)
    return factor_of


def normal_values(own_key, extent, deviation, limit, pieces=(), held_as=jnp.bfloat16):
    values = jax.random.normal(own_key, extent, jnp.float32) * deviation
    if len(pieces) > 0:
        values = level_of(own_key, extent, pieces, -0.22, 0.18) * values
    return jnp.clip(values, min=-limit, max=limit).astype(held_as)


def setup_inputs(seed: int = 0) -> dict:
    streams_of = jax.random.split(jax.random.key(seed), 7)
    return {
        "query_rows": draw_query_rows(jax.random.fold_in(streams_of[6], 71), 0),
        "key_rows": draw_key_rows(jax.random.fold_in(streams_of[6], 71), 0),
        "value_rows": normal_values(streams_of[2], (TOKENS, HEADS, HD), 1.0, 6.0, ((0, 128), (1, 4))),
        "cotangent": normal_values(streams_of[3], (TOKENS, HEADS, HD), 1.0, 6.0, ((0, 128), (1, 4))),
        "norm_gain": jnp.clip(jnp.exp(math.log(2.0) - 1.3862944 * jax.random.uniform(streams_of[4], (HEADS, HD), jnp.float32) ** level_of(streams_of[4], (HEADS, HD), ((0, 4),), -0.2, 0.2)), 0.5, 2.0),
        "offsets": draw_offsets(jax.random.fold_in(streams_of[6], 71), 0),
    }


neg_fill = -1e+30
epsilon = 1e-05

def level_places(offsets, stride):
    seg_len = stride * SEL
    seg_total = TOKENS // seg_len
    starts = jnp.arange(seg_total, dtype=jnp.int32) * seg_len
    inside = stride * jnp.arange(SEL, dtype=jnp.int32)
    shifted = (offsets % stride).astype(jnp.int32)
    return starts[None, :, None] + inside[None, None, :] + shifted[:, None, None]

def reference(query_rows, key_rows, value_rows, cotangent, norm_gain, offsets):
    score_scale = HD ** (-0.5)
    lower = jnp.tril(jnp.ones((SEL, SEL), dtype=bool))
    level_rates = (1, RATE2, RATE3, RATE4)

    def group_scores(query_grp, key_grp):
        raw = jnp.dot(query_grp, key_grp.T, preferred_element_type=jnp.float32) * score_scale
        return jnp.where(lower, raw, neg_fill)

    def group_lse(members):
        scores = group_scores(members[0], members[1])
        row_peak = lax.optimization_barrier(jnp.max(scores, axis=1))
        return row_peak + jnp.log(lax.optimization_barrier(jnp.sum(jnp.exp(scores - row_peak[:, None]), axis=1)))

    def group_out(members):
        scores = group_scores(members[0], members[1])
        weights = jnp.exp(scores - members[3][:, None]).astype(jnp.bfloat16)
        return jnp.dot(weights, members[2], preferred_element_type=jnp.float32)

    def group_grads(members):
        query_grp, key_grp, value_grp, lse_grp, dout_grp, delta_grp = members
        scores = group_scores(query_grp, key_grp)
        weights = jnp.exp(scores - lse_grp[:, None])
        weights_low = weights.astype(jnp.bfloat16)
        value_part = jnp.dot(weights_low.T, dout_grp, preferred_element_type=jnp.float32)
        weight_grad = jnp.dot(dout_grp, value_grp.T, preferred_element_type=jnp.float32)
        score_grad = (weights * (weight_grad - delta_grp[:, None])).astype(jnp.bfloat16)
        query_part = jnp.dot(score_grad, key_grp, preferred_element_type=jnp.float32) * score_scale
        key_part = jnp.dot(score_grad.T, query_grp, preferred_element_type=jnp.float32) * score_scale
        return (query_part, key_part, value_part)
    log_total = jnp.full((TOKENS, HEADS), neg_fill, jnp.float32)
    for stride in level_rates:
        places = level_places(offsets, stride)
        for head in range(HEADS):
            where_rows = places[head]
            flat_rows = where_rows.reshape(-1)
            query_grp = query_rows[:, head][where_rows]
            key_grp = key_rows[:, head][where_rows]
            level_lse = lax.map(group_lse, (query_grp, key_grp))
            log_total = log_total.at[flat_rows, head].set(jnp.logaddexp(log_total[flat_rows, head], level_lse.reshape(-1)))
    attended = jnp.zeros((TOKENS, HEADS, HD), jnp.float32)
    for stride in level_rates:
        places = level_places(offsets, stride)
        for head in range(HEADS):
            where_rows = places[head]
            flat_rows = where_rows.reshape(-1)
            members = (query_rows[:, head][where_rows], key_rows[:, head][where_rows], value_rows[:, head][where_rows], log_total[:, head][where_rows])
            outputs = lax.map(group_out, members)
            attended = attended.at[flat_rows, head].add(outputs.reshape(-1, HD))
    centre = lax.optimization_barrier(jnp.mean(attended, axis=(1, 2)))
    variance = lax.optimization_barrier(jnp.mean(attended * attended, axis=(1, 2))) - centre * centre
    inverse = lax.rsqrt(variance + epsilon)
    normed = (attended - centre[:, None, None]) * inverse[:, None, None]
    grad_in = cotangent.astype(jnp.float32) * norm_gain[None]
    first = lax.optimization_barrier(jnp.mean(grad_in, axis=(1, 2)))
    second = lax.optimization_barrier(jnp.mean(grad_in * normed, axis=(1, 2)))
    d_attended = (inverse[:, None, None] * (grad_in - first[:, None, None] - normed * second[:, None, None])).astype(jnp.bfloat16)
    row_delta = lax.optimization_barrier(jnp.sum(d_attended.astype(jnp.float32) * attended, axis=2))
    query_grad = jnp.zeros((TOKENS, HEADS, HD), jnp.float32)
    key_grad = jnp.zeros((TOKENS, HEADS, HD), jnp.float32)
    value_grad = jnp.zeros((TOKENS, HEADS, HD), jnp.float32)
    for stride in level_rates:
        places = level_places(offsets, stride)
        for head in range(HEADS):
            where_rows = places[head]
            flat_rows = where_rows.reshape(-1)
            members = (query_rows[:, head][where_rows], key_rows[:, head][where_rows], value_rows[:, head][where_rows], log_total[:, head][where_rows], d_attended[:, head][where_rows], row_delta[:, head][where_rows])
            query_part, key_part, value_part = lax.map(group_grads, members)
            query_grad = query_grad.at[flat_rows, head].add(query_part.reshape(-1, HD))
            key_grad = key_grad.at[flat_rows, head].add(key_part.reshape(-1, HD))
            value_grad = value_grad.at[flat_rows, head].add(value_part.reshape(-1, HD))
    return (query_grad.astype(jnp.bfloat16), key_grad.astype(jnp.bfloat16), value_grad.astype(jnp.bfloat16))
```

```python
import numpy as np
import jax
import jax.numpy as jnp
from jax import lax
from jax.sharding import Mesh
from jax.sharding import PartitionSpec as P

RATE2 = 4
RATE3 = 16
RATE4 = 32
RATES = (1, RATE2, RATE3, RATE4)

neg_fill = -1e30
epsilon = 1e-05


def pick_rows(source, wanted, stride):
    row_count = source.shape[0] // stride
    shaped = source.reshape((row_count, stride) + source.shape[1:])
    trailing = (1,) * (source.ndim - 2)
    target = wanted.reshape((1, 1, -1) + trailing)
    column = jnp.arange(stride, dtype=jnp.int32).reshape((1, stride, 1) + trailing)
    zeroed = jnp.where(column == target, shaped, jnp.zeros((), source.dtype))
    return jnp.sum(zeroed, axis=1, dtype=source.dtype)


def put_rows(compact, wanted, stride, filler):
    trailing = (1,) * (compact.ndim - 2)
    target = wanted.reshape((1, 1, -1) + trailing)
    column = jnp.arange(stride, dtype=jnp.int32).reshape((1, stride, 1) + trailing)
    spread = jnp.where(column == target, compact[:, None], jnp.asarray(filler, compact.dtype))
    return spread.reshape((compact.shape[0] * stride,) + compact.shape[1:])


def level_plan(tok_dev, seq_count):
    group_rows = tok_dev * seq_count // RATE4
    spans = [max(1, stride * group_rows // tok_dev) for stride in RATES]
    factors = []
    covered = 1
    for span in spans:
        factors.append(span // covered)
        covered = span
    names = tuple("s%d" % (index + 1) for index in range(len(spans)))
    return spans, factors, names


def shards(plan, query_rows, key_rows, value_rows, cotangent, norm_gain, offsets):
    spans, factors, names = plan
    tok_dev, heads_dev, head_size = query_rows.shape
    score_scale = head_size ** (-0.5)
    features = heads_dev * head_size * lax.axis_size("head")
    seq_axes = tuple(reversed(names))
    device = lax.axis_index(seq_axes)

    levels = []
    for index, stride in enumerate(RATES):
        axes = tuple(reversed(names[: index + 1]))
        span = spans[index]
        rows = tok_dev // stride
        wanted = offsets % stride
        place = (device % span) * rows
        key_sel = pick_rows(key_rows, wanted, stride)
        value_sel = pick_rows(value_rows, wanted, stride)
        query_sel = pick_rows(query_rows, wanted, stride)
        packed = jnp.stack([key_sel, value_sel, query_sel], axis=1)
        gathered = lax.all_gather(packed, axes, axis=0, tiled=True)
        levels.append(
            dict(
                stride=stride,
                axes=axes,
                rows=rows,
                wanted=wanted,
                place=place,
                key_sel=key_sel,
                value_sel=value_sel,
                query_sel=query_sel,
                key_all=gathered[:, 0],
                value_all=gathered[:, 1],
                query_all=gathered[:, 2],
            )
        )

    lse_total = jnp.full((tok_dev, heads_dev), neg_fill, jnp.float32)
    for level in levels:
        total_rows = level["key_all"].shape[0]
        raw = (
            jnp.einsum(
                "qhd,khd->hqk", level["query_sel"], level["key_all"],
                preferred_element_type=jnp.float32,
            )
            * score_scale
        )
        query_at = level["place"] + jnp.arange(level["rows"], dtype=jnp.int32)
        key_at = jnp.arange(total_rows, dtype=jnp.int32)
        linked = key_at[None, :] <= query_at[:, None]
        scores = jnp.where(linked[None], raw, neg_fill)
        row_peak = jnp.max(scores, axis=2)
        level_lse = row_peak + jnp.log(jnp.sum(jnp.exp(scores - row_peak[:, :, None]), axis=2))
        level["scores"] = scores
        lse_total = jnp.logaddexp(
            lse_total, put_rows(level_lse.T, level["wanted"], level["stride"], neg_fill)
        )

    attended = jnp.zeros((tok_dev, heads_dev, head_size), jnp.float32)
    for level in levels:
        lse_sel = pick_rows(lse_total, level["wanted"], level["stride"])
        weights = jnp.exp(level["scores"] - lse_sel.T[:, :, None])
        level["lse_sel"] = lse_sel
        level["weights"] = weights
        out_sel = jnp.einsum(
            "hqk,khd->qhd", weights.astype(jnp.bfloat16), level["value_all"],
            preferred_element_type=jnp.float32,
        )
        attended = attended + put_rows(out_sel, level["wanted"], level["stride"], 0.0)

    grad_in = cotangent.astype(jnp.float32) * norm_gain[None]
    sums = lax.psum(
        jnp.stack(
            [
                jnp.sum(attended, axis=(1, 2)),
                jnp.sum(attended * attended, axis=(1, 2)),
                jnp.sum(grad_in, axis=(1, 2)),
                jnp.sum(grad_in * attended, axis=(1, 2)),
            ]
        ),
        "head",
    )
    centre = sums[0] / features
    variance = sums[1] / features - centre * centre
    inverse = lax.rsqrt(variance + epsilon)
    first_mean = sums[2] / features
    second_mean = inverse * (sums[3] / features - centre * first_mean)
    normed = (attended - centre[:, None, None]) * inverse[:, None, None]
    d_attended = (
        inverse[:, None, None]
        * (grad_in - first_mean[:, None, None] - normed * second_mean[:, None, None])
    ).astype(jnp.bfloat16)
    row_delta = jnp.sum(d_attended.astype(jnp.float32) * attended, axis=2)

    query_grad = jnp.zeros((tok_dev, heads_dev, head_size), jnp.float32)
    for level in levels:
        dout_sel = pick_rows(d_attended, level["wanted"], level["stride"])
        delta_sel = pick_rows(row_delta, level["wanted"], level["stride"])
        weight_grad = jnp.einsum(
            "qhd,khd->hqk", dout_sel, level["value_all"], preferred_element_type=jnp.float32
        )
        score_grad = (level["weights"] * (weight_grad - delta_sel.T[:, :, None])).astype(
            jnp.bfloat16
        )
        grad_sel = jnp.einsum(
            "hqk,khd->qhd", score_grad, level["key_all"], preferred_element_type=jnp.float32
        )
        query_grad = query_grad + put_rows(
            grad_sel * score_scale, level["wanted"], level["stride"], 0.0
        )
        level["dout_all"] = lax.all_gather(dout_sel, level["axes"], axis=0, tiled=True)
        stats = jnp.stack([level["lse_sel"], delta_sel], axis=1)
        level["stats_all"] = lax.all_gather(stats, level["axes"], axis=0, tiled=True)

    key_grad = jnp.zeros((tok_dev, heads_dev, head_size), jnp.float32)
    value_grad = jnp.zeros((tok_dev, heads_dev, head_size), jnp.float32)
    for level in levels:
        query_all = level["query_all"]
        dout_all = level["dout_all"]
        lse_all = level["stats_all"][:, 0]
        delta_all = level["stats_all"][:, 1]
        total_rows = query_all.shape[0]
        raw = (
            jnp.einsum(
                "qhd,khd->hqk", query_all, level["key_sel"], preferred_element_type=jnp.float32
            )
            * score_scale
        )
        key_at = level["place"] + jnp.arange(level["rows"], dtype=jnp.int32)
        query_at = jnp.arange(total_rows, dtype=jnp.int32)
        linked = key_at[None, :] <= query_at[:, None]
        scores = jnp.where(linked[None], raw, neg_fill)
        weights = jnp.exp(scores - lse_all.T[:, :, None])
        value_grad_sel = jnp.einsum(
            "hqk,qhd->khd", weights.astype(jnp.bfloat16), dout_all,
            preferred_element_type=jnp.float32,
        )
        weight_grad = jnp.einsum(
            "qhd,khd->hqk", dout_all, level["value_sel"], preferred_element_type=jnp.float32
        )
        score_grad = (weights * (weight_grad - delta_all.T[:, :, None])).astype(jnp.bfloat16)
        key_grad_sel = jnp.einsum(
            "hqk,qhd->khd", score_grad, query_all, preferred_element_type=jnp.float32
        )
        key_grad = key_grad + put_rows(
            key_grad_sel * score_scale, level["wanted"], level["stride"], 0.0
        )
        value_grad = value_grad + put_rows(value_grad_sel, level["wanted"], level["stride"], 0.0)

    return (
        query_grad.astype(jnp.bfloat16),
        key_grad.astype(jnp.bfloat16),
        value_grad.astype(jnp.bfloat16),
    )


def solution(mesh):
    seq_count = mesh.shape["seq"]
    head_count = mesh.shape["head"]

    def run(query_rows, key_rows, value_rows, cotangent, norm_gain, offsets):
        tok_dev = query_rows.shape[0] // seq_count
        plan = level_plan(tok_dev, seq_count)
        spans, factors, names = plan
        grid = np.asarray(mesh.devices).reshape(tuple(reversed(factors)) + (head_count,))
        sub_mesh = Mesh(grid, tuple(reversed(names)) + ("head",))
        seq_spec = tuple(reversed(names))
        rows_spec = P(seq_spec, "head", None)
        placed = (rows_spec, rows_spec, rows_spec, rows_spec, P("head", None), P("head"))

        def body(*args):
            return shards(plan, *args)

        return jax.shard_map(
            body,
            mesh=sub_mesh,
            in_specs=placed,
            out_specs=(rows_spec, rows_spec, rows_spec),
            check_vma=False,
        )(query_rows, key_rows, value_rows, cotangent, norm_gain, offsets)

    return run
```

```python
import jax
import jax.numpy as jnp
from jax import lax
from jax.sharding import PartitionSpec as P

RATE2 = 4
RATE3 = 16
RATE4 = 32
RATES = (1, RATE2, RATE3, RATE4)

neg_fill = -1e30
epsilon = 1e-05
lane = 128


def passed_along(value, axis, steps):
    count = lax.axis_size(axis)
    leading, last = (max(0, -steps), min(count, count - steps))
    return lax.ppermute(value, axis, [(source, source + steps) for source in range(leading, last)])


def pick_rows(source, wanted, stride):
    row_count = source.shape[0] // stride
    shaped = source.reshape((row_count, stride) + source.shape[1:])
    trailing = (1,) * (source.ndim - 2)
    target = wanted.reshape((1, 1, -1) + trailing)
    column = jnp.arange(stride, dtype=jnp.int32).reshape((1, stride, 1) + trailing)
    zeroed = jnp.where(column == target, shaped, jnp.zeros((), source.dtype))
    return jnp.sum(zeroed, axis=1, dtype=source.dtype)


def put_rows(compact, wanted, stride, filler):
    trailing = (1,) * (compact.ndim - 2)
    target = wanted.reshape((1, 1, -1) + trailing)
    column = jnp.arange(stride, dtype=jnp.int32).reshape((1, stride, 1) + trailing)
    spread = jnp.where(column == target, compact[:, None], jnp.asarray(filler, compact.dtype))
    return spread.reshape((compact.shape[0] * stride,) + compact.shape[1:])


def pull(arrays, steps):
    flat = [held.reshape(-1, lane) for held in arrays]
    sizes = [piece.shape[0] for piece in flat]
    moved = passed_along(jnp.concatenate(flat, axis=0), "seq", steps)
    out = []
    start = 0
    for held, size in zip(arrays, sizes):
        out.append(moved[start : start + size].reshape(held.shape))
        start += size
    return out


def extend(sets, spans, sign):
    sets = [list(members) for members in sets]
    covered = 1
    while covered < max(spans):
        active = [index for index, span in enumerate(spans) if span > covered]
        arrived = pull([held for index in active for held in sets[index]], sign * covered)
        taken = 0
        for index in active:
            count = len(sets[index])
            sets[index] = [
                jnp.concatenate([held, current], axis=0)
                for held, current in zip(sets[index], arrived[taken : taken + count])
            ]
            taken += count
        covered *= 2
    return [[held[:span] for held in members] for members, span in zip(sets, spans)]


def split_exact(value):
    high = lax.reduce_precision(value, exponent_bits=8, mantissa_bits=7)
    rest = value - high
    middle = lax.reduce_precision(rest, exponent_bits=8, mantissa_bits=7)
    low = rest - middle
    return jnp.stack([high, middle, low], axis=-1).astype(jnp.bfloat16)


def join_exact(parts):
    parts = parts.astype(jnp.float32)
    return (parts[..., 0] + parts[..., 1]) + parts[..., 2]


def pack_stats(lse_sel, delta_sel):
    coded = split_exact(jnp.stack([lse_sel, delta_sel], axis=-1)).reshape(-1)
    padded = -(-coded.shape[0] // lane) * lane
    coded = jnp.pad(coded, (0, padded - coded.shape[0]))
    return coded.reshape(1, padded // lane, lane)


def unpack_stats(coded, rows, heads_dev):
    slots = coded.shape[0]
    flat = coded.reshape(slots, -1)[:, : rows * heads_dev * 6]
    values = join_exact(flat.reshape(slots * rows, heads_dev, 2, 3))
    return values[:, :, 0], values[:, :, 1]


def shards(query_rows, key_rows, value_rows, cotangent, norm_gain, offsets):
    tok_dev, heads_dev, head_size = query_rows.shape
    seq_count = lax.axis_size("seq")
    device = lax.axis_index("seq")
    group_rows = tok_dev * seq_count // RATE4
    score_scale = head_size ** (-0.5)
    features = heads_dev * head_size * lax.axis_size("head")

    levels = []
    for stride in RATES:
        span = max(1, stride * group_rows // tok_dev)
        rows = tok_dev // stride
        wanted = offsets % stride
        levels.append(
            dict(
                stride=stride,
                span=span,
                rows=rows,
                wanted=wanted,
                spot=device % span,
                key_sel=pick_rows(key_rows, wanted, stride),
                value_sel=pick_rows(value_rows, wanted, stride),
                query_sel=pick_rows(query_rows, wanted, stride),
            )
        )
    spans = [level["span"] for level in levels]

    key_sets = extend(
        [[level["key_sel"][None], level["value_sel"][None]] for level in levels], spans, 1
    )
    query_sets = extend([[level["query_sel"][None]] for level in levels], spans, -1)

    lse_total = jnp.full((tok_dev, heads_dev), neg_fill, jnp.float32)
    for level, (key_set, value_set) in zip(levels, key_sets):
        span, rows = level["span"], level["rows"]
        keys = key_set.reshape(span * rows, heads_dev, head_size)
        level["key_all"] = keys
        level["value_all"] = value_set.reshape(span * rows, heads_dev, head_size)
        raw = (
            jnp.einsum("qhd,khd->hqk", level["query_sel"], keys, preferred_element_type=jnp.float32)
            * score_scale
        )
        flat_at = jnp.arange(span * rows, dtype=jnp.int32)
        slot = (flat_at // rows)[None, :]
        key_row = (flat_at % rows)[None, :]
        query_row = jnp.arange(rows, dtype=jnp.int32)[:, None]
        linked = (slot <= level["spot"]) & ((slot > 0) | (key_row <= query_row))
        scores = jnp.where(linked[None], raw, neg_fill)
        row_peak = jnp.max(scores, axis=2)
        level_lse = row_peak + jnp.log(jnp.sum(jnp.exp(scores - row_peak[:, :, None]), axis=2))
        level["scores"] = scores
        lse_total = jnp.logaddexp(
            lse_total, put_rows(level_lse.T, level["wanted"], level["stride"], neg_fill)
        )

    attended = jnp.zeros((tok_dev, heads_dev, head_size), jnp.float32)
    for level in levels:
        lse_sel = pick_rows(lse_total, level["wanted"], level["stride"])
        weights = jnp.exp(level["scores"] - lse_sel.T[:, :, None])
        level["lse_sel"] = lse_sel
        level["weights"] = weights
        out_sel = jnp.einsum(
            "hqk,khd->qhd", weights.astype(jnp.bfloat16), level["value_all"],
            preferred_element_type=jnp.float32,
        )
        attended = attended + put_rows(out_sel, level["wanted"], level["stride"], 0.0)

    grad_in = cotangent.astype(jnp.float32) * norm_gain[None]
    sums = lax.psum(
        jnp.stack(
            [
                jnp.sum(attended, axis=(1, 2)),
                jnp.sum(attended * attended, axis=(1, 2)),
                jnp.sum(grad_in, axis=(1, 2)),
                jnp.sum(grad_in * attended, axis=(1, 2)),
            ]
        ),
        "head",
    )
    centre = sums[0] / features
    variance = sums[1] / features - centre * centre
    inverse = lax.rsqrt(variance + epsilon)
    first_mean = sums[2] / features
    second_mean = inverse * (sums[3] / features - centre * first_mean)
    normed = (attended - centre[:, None, None]) * inverse[:, None, None]
    d_attended = (
        inverse[:, None, None]
        * (grad_in - first_mean[:, None, None] - normed * second_mean[:, None, None])
    ).astype(jnp.bfloat16)
    row_delta = jnp.sum(d_attended.astype(jnp.float32) * attended, axis=2)

    query_grad = jnp.zeros((tok_dev, heads_dev, head_size), jnp.float32)
    back_sets = []
    for level in levels:
        dout_sel = pick_rows(d_attended, level["wanted"], level["stride"])
        delta_sel = pick_rows(row_delta, level["wanted"], level["stride"])
        back_sets.append([dout_sel[None], pack_stats(level["lse_sel"], delta_sel)])
        weight_grad = jnp.einsum(
            "qhd,khd->hqk", dout_sel, level["value_all"], preferred_element_type=jnp.float32
        )
        score_grad = (level["weights"] * (weight_grad - delta_sel.T[:, :, None])).astype(
            jnp.bfloat16
        )
        grad_sel = jnp.einsum(
            "hqk,khd->qhd", score_grad, level["key_all"], preferred_element_type=jnp.float32
        )
        query_grad = query_grad + put_rows(
            grad_sel * score_scale, level["wanted"], level["stride"], 0.0
        )
    back_sets = extend(back_sets, spans, -1)

    key_grad = jnp.zeros((tok_dev, heads_dev, head_size), jnp.float32)
    value_grad = jnp.zeros((tok_dev, heads_dev, head_size), jnp.float32)
    for level, (query_set,), (dout_set, stats_set) in zip(levels, query_sets, back_sets):
        span, rows = level["span"], level["rows"]
        queries = query_set.reshape(span * rows, heads_dev, head_size)
        dout_all = dout_set.reshape(span * rows, heads_dev, head_size)
        lse_all, delta_all = unpack_stats(stats_set, rows, heads_dev)
        raw = (
            jnp.einsum(
                "qhd,khd->hqk", queries, level["key_sel"], preferred_element_type=jnp.float32
            )
            * score_scale
        )
        flat_at = jnp.arange(span * rows, dtype=jnp.int32)
        slot = (flat_at // rows)[:, None]
        query_row = (flat_at % rows)[:, None]
        key_row = jnp.arange(rows, dtype=jnp.int32)[None, :]
        linked = (slot < span - level["spot"]) & ((slot > 0) | (query_row >= key_row))
        scores = jnp.where(linked[None], raw, neg_fill)
        weights = jnp.exp(scores - lse_all.T[:, :, None])
        value_grad_sel = jnp.einsum(
            "hqk,qhd->khd", weights.astype(jnp.bfloat16), dout_all,
            preferred_element_type=jnp.float32,
        )
        weight_grad = jnp.einsum(
            "qhd,khd->hqk", dout_all, level["value_sel"], preferred_element_type=jnp.float32
        )
        score_grad = (weights * (weight_grad - delta_all.T[:, :, None])).astype(jnp.bfloat16)
        key_grad_sel = jnp.einsum(
            "hqk,qhd->khd", score_grad, queries, preferred_element_type=jnp.float32
        )
        key_grad = key_grad + put_rows(
            key_grad_sel * score_scale, level["wanted"], level["stride"], 0.0
        )
        value_grad = value_grad + put_rows(value_grad_sel, level["wanted"], level["stride"], 0.0)

    return (
        query_grad.astype(jnp.bfloat16),
        key_grad.astype(jnp.bfloat16),
        value_grad.astype(jnp.bfloat16),
    )


def solution(mesh):
    placed = (
        P("seq", "head", None),
        P("seq", "head", None),
        P("seq", "head", None),
        P("seq", "head", None),
        P("head", None),
        P("head"),
    )
    return jax.shard_map(
        shards,
        mesh=mesh,
        in_specs=placed,
        out_specs=(P("seq", "head", None), P("seq", "head", None), P("seq", "head", None)),
        check_vma=False,
    )
```

```python
import jax
import jax.numpy as jnp
from jax import lax
from jax.sharding import PartitionSpec as P

RATE2 = 4
RATE3 = 16
RATE4 = 32
RATES = (1, RATE2, RATE3, RATE4)

neg_fill = -1e30
epsilon = 1e-05
lane = 128


def passed_along(value, axis, steps):
    count = lax.axis_size(axis)
    leading, last = (max(0, -steps), min(count, count - steps))
    return lax.ppermute(value, axis, [(source, source + steps) for source in range(leading, last)])


def pick_rows(source, wanted, stride):
    row_count = source.shape[0] // stride
    shaped = source.reshape((row_count, stride) + source.shape[1:])
    trailing = (1,) * (source.ndim - 2)
    target = wanted.reshape((1, 1, -1) + trailing)
    column = jnp.arange(stride, dtype=jnp.int32).reshape((1, stride, 1) + trailing)
    zeroed = jnp.where(column == target, shaped, jnp.zeros((), source.dtype))
    return jnp.sum(zeroed, axis=1, dtype=source.dtype)


def put_rows(compact, wanted, stride, filler):
    trailing = (1,) * (compact.ndim - 2)
    target = wanted.reshape((1, 1, -1) + trailing)
    column = jnp.arange(stride, dtype=jnp.int32).reshape((1, stride, 1) + trailing)
    spread = jnp.where(column == target, compact[:, None], jnp.asarray(filler, compact.dtype))
    return spread.reshape((compact.shape[0] * stride,) + compact.shape[1:])


def extend(buffers, spans, sign):
    buffers = list(buffers)
    slot_rows = [held.shape[0] for held in buffers]
    covered = 1
    while covered < max(spans):
        active = [index for index, span in enumerate(spans) if span > covered]
        moved = passed_along(
            jnp.concatenate([buffers[index] for index in active], axis=0), "seq", sign * covered
        )
        start = 0
        for index in active:
            size = buffers[index].shape[0]
            buffers[index] = jnp.concatenate(
                [buffers[index], moved[start : start + size]], axis=0
            )
            start += size
        covered *= 2
    return [held[: span * size] for held, span, size in zip(buffers, spans, slot_rows)]


def split_exact(value):
    high = lax.reduce_precision(value, exponent_bits=8, mantissa_bits=7)
    rest = value - high
    middle = lax.reduce_precision(rest, exponent_bits=8, mantissa_bits=7)
    low = rest - middle
    return jnp.stack([high, middle, low], axis=-1).astype(jnp.bfloat16)


def join_exact(parts):
    parts = parts.astype(jnp.float32)
    return (parts[..., 0] + parts[..., 1]) + parts[..., 2]


def stats_rows(rows, heads_dev):
    return -(-(rows * heads_dev * 6) // (16 * lane)) * 16


def pack_stats(lse_sel, delta_sel):
    rows, heads_dev = lse_sel.shape
    coded = split_exact(jnp.stack([lse_sel, delta_sel], axis=-1)).reshape(-1)
    padded = stats_rows(rows, heads_dev) * lane
    coded = jnp.pad(coded, (0, padded - coded.shape[0]))
    return coded.reshape(padded // lane, lane)


def unpack_stats(coded, slots, rows, heads_dev):
    flat = coded.reshape(slots, -1)[:, : rows * heads_dev * 6]
    values = join_exact(flat.reshape(slots * rows, heads_dev, 2, 3))
    return values[:, :, 0], values[:, :, 1]


def shards(query_rows, key_rows, value_rows, cotangent, norm_gain, offsets):
    tok_dev, heads_dev, head_size = query_rows.shape
    seq_count = lax.axis_size("seq")
    device = lax.axis_index("seq")
    group_rows = tok_dev * seq_count // RATE4
    score_scale = head_size ** (-0.5)
    features = heads_dev * head_size * lax.axis_size("head")

    levels = []
    for stride in RATES:
        span = max(1, stride * group_rows // tok_dev)
        rows = tok_dev // stride
        wanted = offsets % stride
        levels.append(
            dict(
                stride=stride,
                span=span,
                rows=rows,
                wanted=wanted,
                spot=device % span,
                key_sel=pick_rows(key_rows, wanted, stride),
                value_sel=pick_rows(value_rows, wanted, stride),
                query_sel=pick_rows(query_rows, wanted, stride),
            )
        )
    spans = [level["span"] for level in levels]

    key_sets = extend(
        [
            jnp.concatenate(
                [
                    level["key_sel"].reshape(-1, lane),
                    level["value_sel"].reshape(-1, lane),
                ],
                axis=0,
            )
            for level in levels
        ],
        spans,
        1,
    )
    query_sets = extend([level["query_sel"].reshape(-1, lane) for level in levels], spans, -1)

    lse_total = jnp.full((tok_dev, heads_dev), neg_fill, jnp.float32)
    for level, key_set in zip(levels, key_sets):
        span, rows = level["span"], level["rows"]
        paired = key_set.reshape(span, 2, rows, heads_dev, head_size)
        keys = paired[:, 0].reshape(span * rows, heads_dev, head_size)
        level["key_all"] = keys
        level["value_all"] = paired[:, 1].reshape(span * rows, heads_dev, head_size)
        raw = (
            jnp.einsum("qhd,khd->hqk", level["query_sel"], keys, preferred_element_type=jnp.float32)
            * score_scale
        )
        flat_at = jnp.arange(span * rows, dtype=jnp.int32)
        slot = (flat_at // rows)[None, :]
        key_row = (flat_at % rows)[None, :]
        query_row = jnp.arange(rows, dtype=jnp.int32)[:, None]
        linked = (slot <= level["spot"]) & ((slot > 0) | (key_row <= query_row))
        scores = jnp.where(linked[None], raw, neg_fill)
        row_peak = jnp.max(scores, axis=2)
        level_lse = row_peak + jnp.log(jnp.sum(jnp.exp(scores - row_peak[:, :, None]), axis=2))
        level["scores"] = scores
        lse_total = jnp.logaddexp(
            lse_total, put_rows(level_lse.T, level["wanted"], level["stride"], neg_fill)
        )

    attended = jnp.zeros((tok_dev, heads_dev, head_size), jnp.float32)
    for level in levels:
        lse_sel = pick_rows(lse_total, level["wanted"], level["stride"])
        weights = jnp.exp(level["scores"] - lse_sel.T[:, :, None])
        level["lse_sel"] = lse_sel
        level["weights"] = weights
        out_sel = jnp.einsum(
            "hqk,khd->qhd", weights.astype(jnp.bfloat16), level["value_all"],
            preferred_element_type=jnp.float32,
        )
        attended = attended + put_rows(out_sel, level["wanted"], level["stride"], 0.0)

    grad_in = cotangent.astype(jnp.float32) * norm_gain[None]
    sums = lax.psum(
        jnp.stack(
            [
                jnp.sum(attended, axis=(1, 2)),
                jnp.sum(attended * attended, axis=(1, 2)),
                jnp.sum(grad_in, axis=(1, 2)),
                jnp.sum(grad_in * attended, axis=(1, 2)),
            ]
        ),
        "head",
    )
    centre = sums[0] / features
    variance = sums[1] / features - centre * centre
    inverse = lax.rsqrt(variance + epsilon)
    first_mean = sums[2] / features
    second_mean = inverse * (sums[3] / features - centre * first_mean)
    normed = (attended - centre[:, None, None]) * inverse[:, None, None]
    d_attended = (
        inverse[:, None, None]
        * (grad_in - first_mean[:, None, None] - normed * second_mean[:, None, None])
    ).astype(jnp.bfloat16)
    row_delta = jnp.sum(d_attended.astype(jnp.float32) * attended, axis=2)

    query_grad = jnp.zeros((tok_dev, heads_dev, head_size), jnp.float32)
    back_sets = []
    for level in levels:
        dout_sel = pick_rows(d_attended, level["wanted"], level["stride"])
        delta_sel = pick_rows(row_delta, level["wanted"], level["stride"])
        back_sets.append(
            jnp.concatenate(
                [dout_sel.reshape(-1, lane), pack_stats(level["lse_sel"], delta_sel)], axis=0
            )
        )
        weight_grad = jnp.einsum(
            "qhd,khd->hqk", dout_sel, level["value_all"], preferred_element_type=jnp.float32
        )
        score_grad = (level["weights"] * (weight_grad - delta_sel.T[:, :, None])).astype(
            jnp.bfloat16
        )
        grad_sel = jnp.einsum(
            "hqk,khd->qhd", score_grad, level["key_all"], preferred_element_type=jnp.float32
        )
        query_grad = query_grad + put_rows(
            grad_sel * score_scale, level["wanted"], level["stride"], 0.0
        )
    back_sets = extend(back_sets, spans, -1)

    key_grad = jnp.zeros((tok_dev, heads_dev, head_size), jnp.float32)
    value_grad = jnp.zeros((tok_dev, heads_dev, head_size), jnp.float32)
    for level, query_set, back_set in zip(levels, query_sets, back_sets):
        span, rows = level["span"], level["rows"]
        queries = query_set.reshape(span * rows, heads_dev, head_size)
        back_slots = back_set.reshape(span, -1, lane)
        dout_all = back_slots[:, : rows * heads_dev].reshape(span * rows, heads_dev, head_size)
        lse_all, delta_all = unpack_stats(
            back_slots[:, rows * heads_dev :], span, rows, heads_dev
        )
        raw = (
            jnp.einsum(
                "qhd,khd->hqk", queries, level["key_sel"], preferred_element_type=jnp.float32
            )
            * score_scale
        )
        flat_at = jnp.arange(span * rows, dtype=jnp.int32)
        slot = (flat_at // rows)[:, None]
        query_row = (flat_at % rows)[:, None]
        key_row = jnp.arange(rows, dtype=jnp.int32)[None, :]
        linked = (slot < span - level["spot"]) & ((slot > 0) | (query_row >= key_row))
        scores = jnp.where(linked[None], raw, neg_fill)
        weights = jnp.exp(scores - lse_all.T[:, :, None])
        value_grad_sel = jnp.einsum(
            "hqk,qhd->khd", weights.astype(jnp.bfloat16), dout_all,
            preferred_element_type=jnp.float32,
        )
        weight_grad = jnp.einsum(
            "qhd,khd->hqk", dout_all, level["value_sel"], preferred_element_type=jnp.float32
        )
        score_grad = (weights * (weight_grad - delta_all.T[:, :, None])).astype(jnp.bfloat16)
        key_grad_sel = jnp.einsum(
            "hqk,qhd->khd", score_grad, queries, preferred_element_type=jnp.float32
        )
        key_grad = key_grad + put_rows(
            key_grad_sel * score_scale, level["wanted"], level["stride"], 0.0
        )
        value_grad = value_grad + put_rows(value_grad_sel, level["wanted"], level["stride"], 0.0)

    return (
        query_grad.astype(jnp.bfloat16),
        key_grad.astype(jnp.bfloat16),
        value_grad.astype(jnp.bfloat16),
    )


def solution(mesh):
    placed = (
        P("seq", "head", None),
        P("seq", "head", None),
        P("seq", "head", None),
        P("seq", "head", None),
        P("head", None),
        P("head"),
    )
    return jax.shard_map(
        shards,
        mesh=mesh,
        in_specs=placed,
        out_specs=(P("seq", "head", None), P("seq", "head", None), P("seq", "head", None)),
        check_vma=False,
    )
```

```python
import jax
import jax.numpy as jnp
from jax import lax
from jax.sharding import PartitionSpec as P

RATE2 = 4
RATE3 = 16
RATE4 = 32
RATES = (1, RATE2, RATE3, RATE4)

neg_fill = -1e30
epsilon = 1e-05
lane = 128


def passed_along(value, axis, steps):
    count = lax.axis_size(axis)
    leading, last = (max(0, -steps), min(count, count - steps))
    return lax.ppermute(value, axis, [(source, source + steps) for source in range(leading, last)])


def pick_rows(source, wanted, stride):
    row_count = source.shape[0] // stride
    shaped = source.reshape((row_count, stride) + source.shape[1:])
    trailing = (1,) * (source.ndim - 2)
    target = wanted.reshape((1, 1, -1) + trailing)
    column = jnp.arange(stride, dtype=jnp.int32).reshape((1, stride, 1) + trailing)
    zeroed = jnp.where(column == target, shaped, jnp.zeros((), source.dtype))
    return jnp.sum(zeroed, axis=1, dtype=source.dtype)


def put_rows(compact, wanted, stride, filler):
    trailing = (1,) * (compact.ndim - 2)
    target = wanted.reshape((1, 1, -1) + trailing)
    column = jnp.arange(stride, dtype=jnp.int32).reshape((1, stride, 1) + trailing)
    spread = jnp.where(column == target, compact[:, None], jnp.asarray(filler, compact.dtype))
    return spread.reshape((compact.shape[0] * stride,) + compact.shape[1:])


def extend(parts, spans, sign):
    live = sorted(range(len(parts)), key=lambda index: -spans[index])
    sizes = [part.shape[0] for part in parts]
    state = jnp.concatenate([parts[index] for index in live], axis=0)[None]
    finished = {}
    covered = 1
    while live:
        while live and spans[live[-1]] <= covered:
            index = live.pop()
            start = sum(sizes[other] for other in live)
            finished[index] = state[:, start : start + sizes[index]]
            state = state[:, :start]
        if not live:
            break
        moved = passed_along(state, "seq", sign * covered)
        state = jnp.concatenate([state, moved], axis=0)
        covered *= 2
    return [finished[index][: spans[index]] for index in range(len(parts))]


def split_exact(value):
    high = lax.reduce_precision(value, exponent_bits=8, mantissa_bits=7)
    rest = value - high
    middle = lax.reduce_precision(rest, exponent_bits=8, mantissa_bits=7)
    low = rest - middle
    return jnp.stack([high, middle, low], axis=-1).astype(jnp.bfloat16)


def join_exact(parts):
    parts = parts.astype(jnp.float32)
    return (parts[..., 0] + parts[..., 1]) + parts[..., 2]


def stats_rows(rows, heads_dev):
    return -(-(rows * heads_dev * 6) // (16 * lane)) * 16


def pack_stats(lse_sel, delta_sel):
    rows, heads_dev = lse_sel.shape
    coded = split_exact(jnp.stack([lse_sel, delta_sel], axis=-1)).reshape(-1)
    padded = stats_rows(rows, heads_dev) * lane
    coded = jnp.pad(coded, (0, padded - coded.shape[0]))
    return coded.reshape(padded // lane, lane)


def unpack_stats(coded, slots, rows, heads_dev):
    flat = coded.reshape(slots, -1)[:, : rows * heads_dev * 6]
    values = join_exact(flat.reshape(slots * rows, heads_dev, 2, 3))
    return values[:, :, 0], values[:, :, 1]


def shards(query_rows, key_rows, value_rows, cotangent, norm_gain, offsets):
    tok_dev, heads_dev, head_size = query_rows.shape
    seq_count = lax.axis_size("seq")
    device = lax.axis_index("seq")
    group_rows = tok_dev * seq_count // RATE4
    score_scale = head_size ** (-0.5)
    features = heads_dev * head_size * lax.axis_size("head")

    levels = []
    for stride in RATES:
        span = max(1, stride * group_rows // tok_dev)
        rows = tok_dev // stride
        wanted = offsets % stride
        levels.append(
            dict(
                stride=stride,
                span=span,
                rows=rows,
                wanted=wanted,
                spot=device % span,
                key_sel=pick_rows(key_rows, wanted, stride),
                value_sel=pick_rows(value_rows, wanted, stride),
                query_sel=pick_rows(query_rows, wanted, stride),
            )
        )
    spans = [level["span"] for level in levels]

    key_sets = extend(
        [
            jnp.concatenate(
                [
                    level["key_sel"].reshape(-1, lane),
                    level["value_sel"].reshape(-1, lane),
                ],
                axis=0,
            )
            for level in levels
        ],
        spans,
        1,
    )
    query_sets = extend([level["query_sel"].reshape(-1, lane) for level in levels], spans, -1)

    lse_total = jnp.full((tok_dev, heads_dev), neg_fill, jnp.float32)
    for level, key_set in zip(levels, key_sets):
        span, rows = level["span"], level["rows"]
        paired = key_set.reshape(span, 2, rows, heads_dev, head_size)
        keys = paired[:, 0].reshape(span * rows, heads_dev, head_size)
        level["key_all"] = keys
        level["value_all"] = paired[:, 1].reshape(span * rows, heads_dev, head_size)
        raw = (
            jnp.einsum("qhd,khd->hqk", level["query_sel"], keys, preferred_element_type=jnp.float32)
            * score_scale
        )
        flat_at = jnp.arange(span * rows, dtype=jnp.int32)
        slot = (flat_at // rows)[None, :]
        key_row = (flat_at % rows)[None, :]
        query_row = jnp.arange(rows, dtype=jnp.int32)[:, None]
        linked = (slot <= level["spot"]) & ((slot > 0) | (key_row <= query_row))
        scores = jnp.where(linked[None], raw, neg_fill)
        row_peak = jnp.max(scores, axis=2)
        level_lse = row_peak + jnp.log(jnp.sum(jnp.exp(scores - row_peak[:, :, None]), axis=2))
        level["scores"] = scores
        lse_total = jnp.logaddexp(
            lse_total, put_rows(level_lse.T, level["wanted"], level["stride"], neg_fill)
        )

    attended = jnp.zeros((tok_dev, heads_dev, head_size), jnp.float32)
    for level in levels:
        lse_sel = pick_rows(lse_total, level["wanted"], level["stride"])
        weights = jnp.exp(level["scores"] - lse_sel.T[:, :, None])
        level["lse_sel"] = lse_sel
        level["weights"] = weights
        out_sel = jnp.einsum(
            "hqk,khd->qhd", weights.astype(jnp.bfloat16), level["value_all"],
            preferred_element_type=jnp.float32,
        )
        attended = attended + put_rows(out_sel, level["wanted"], level["stride"], 0.0)

    grad_in = cotangent.astype(jnp.float32) * norm_gain[None]
    sums = lax.psum(
        jnp.stack(
            [
                jnp.sum(attended, axis=(1, 2)),
                jnp.sum(attended * attended, axis=(1, 2)),
                jnp.sum(grad_in, axis=(1, 2)),
                jnp.sum(grad_in * attended, axis=(1, 2)),
            ]
        ),
        "head",
    )
    centre = sums[0] / features
    variance = sums[1] / features - centre * centre
    inverse = lax.rsqrt(variance + epsilon)
    first_mean = sums[2] / features
    second_mean = inverse * (sums[3] / features - centre * first_mean)
    normed = (attended - centre[:, None, None]) * inverse[:, None, None]
    d_attended = (
        inverse[:, None, None]
        * (grad_in - first_mean[:, None, None] - normed * second_mean[:, None, None])
    ).astype(jnp.bfloat16)
    row_delta = jnp.sum(d_attended.astype(jnp.float32) * attended, axis=2)

    query_grad = jnp.zeros((tok_dev, heads_dev, head_size), jnp.float32)
    back_sets = []
    for level in levels:
        dout_sel = pick_rows(d_attended, level["wanted"], level["stride"])
        delta_sel = pick_rows(row_delta, level["wanted"], level["stride"])
        back_sets.append(
            jnp.concatenate(
                [dout_sel.reshape(-1, lane), pack_stats(level["lse_sel"], delta_sel)], axis=0
            )
        )
        weight_grad = jnp.einsum(
            "qhd,khd->hqk", dout_sel, level["value_all"], preferred_element_type=jnp.float32
        )
        score_grad = (level["weights"] * (weight_grad - delta_sel.T[:, :, None])).astype(
            jnp.bfloat16
        )
        grad_sel = jnp.einsum(
            "hqk,khd->qhd", score_grad, level["key_all"], preferred_element_type=jnp.float32
        )
        query_grad = query_grad + put_rows(
            grad_sel * score_scale, level["wanted"], level["stride"], 0.0
        )
    back_sets = extend(back_sets, spans, -1)

    key_grad = jnp.zeros((tok_dev, heads_dev, head_size), jnp.float32)
    value_grad = jnp.zeros((tok_dev, heads_dev, head_size), jnp.float32)
    for level, query_set, back_set in zip(levels, query_sets, back_sets):
        span, rows = level["span"], level["rows"]
        queries = query_set.reshape(span * rows, heads_dev, head_size)
        back_slots = back_set.reshape(span, -1, lane)
        dout_all = back_slots[:, : rows * heads_dev].reshape(span * rows, heads_dev, head_size)
        lse_all, delta_all = unpack_stats(
            back_slots[:, rows * heads_dev :], span, rows, heads_dev
        )
        raw = (
            jnp.einsum(
                "qhd,khd->hqk", queries, level["key_sel"], preferred_element_type=jnp.float32
            )
            * score_scale
        )
        flat_at = jnp.arange(span * rows, dtype=jnp.int32)
        slot = (flat_at // rows)[:, None]
        query_row = (flat_at % rows)[:, None]
        key_row = jnp.arange(rows, dtype=jnp.int32)[None, :]
        linked = (slot < span - level["spot"]) & ((slot > 0) | (query_row >= key_row))
        scores = jnp.where(linked[None], raw, neg_fill)
        weights = jnp.exp(scores - lse_all.T[:, :, None])
        value_grad_sel = jnp.einsum(
            "hqk,qhd->khd", weights.astype(jnp.bfloat16), dout_all,
            preferred_element_type=jnp.float32,
        )
        weight_grad = jnp.einsum(
            "qhd,khd->hqk", dout_all, level["value_sel"], preferred_element_type=jnp.float32
        )
        score_grad = (weights * (weight_grad - delta_all.T[:, :, None])).astype(jnp.bfloat16)
        key_grad_sel = jnp.einsum(
            "hqk,qhd->khd", score_grad, queries, preferred_element_type=jnp.float32
        )
        key_grad = key_grad + put_rows(
            key_grad_sel * score_scale, level["wanted"], level["stride"], 0.0
        )
        value_grad = value_grad + put_rows(value_grad_sel, level["wanted"], level["stride"], 0.0)

    return (
        query_grad.astype(jnp.bfloat16),
        key_grad.astype(jnp.bfloat16),
        value_grad.astype(jnp.bfloat16),
    )


def solution(mesh):
    placed = (
        P("seq", "head", None),
        P("seq", "head", None),
        P("seq", "head", None),
        P("seq", "head", None),
        P("head", None),
        P("head"),
    )
    return jax.shard_map(
        shards,
        mesh=mesh,
        in_specs=placed,
        out_specs=(P("seq", "head", None), P("seq", "head", None), P("seq", "head", None)),
        check_vma=False,
    )
```

```python
import numpy as np
import jax
import jax.numpy as jnp
from jax import lax
from jax.sharding import PartitionSpec as P

RATE2 = 4
RATE3 = 16
RATE4 = 32
RATES = (1, RATE2, RATE3, RATE4)

neg_fill = -1e30
epsilon = 1e-05
lane = 128


def pick_rows(source, wanted, stride):
    row_count = source.shape[0] // stride
    shaped = source.reshape((row_count, stride) + source.shape[1:])
    trailing = (1,) * (source.ndim - 2)
    target = wanted.reshape((1, 1, -1) + trailing)
    column = jnp.arange(stride, dtype=jnp.int32).reshape((1, stride, 1) + trailing)
    zeroed = jnp.where(column == target, shaped, jnp.zeros((), source.dtype))
    return jnp.sum(zeroed, axis=1, dtype=source.dtype)


def put_rows(compact, wanted, stride, filler):
    trailing = (1,) * (compact.ndim - 2)
    target = wanted.reshape((1, 1, -1) + trailing)
    column = jnp.arange(stride, dtype=jnp.int32).reshape((1, stride, 1) + trailing)
    spread = jnp.where(column == target, compact[:, None], jnp.asarray(filler, compact.dtype))
    return spread.reshape((compact.shape[0] * stride,) + compact.shape[1:])


def exchange_order(count):
    bits = [1 << bit for bit in range(max(0, (count - 1).bit_length()))]
    order = []
    for first in range(0, len(bits), 2):
        order.extend(reversed(bits[first : first + 2]))
    return order


def spread(order, slots):
    table = np.zeros(slots, np.int32)
    for slot in range(slots):
        for bit, offset in enumerate(order):
            if slot >> bit & 1:
                table[slot] ^= offset
    return table


def extend(parts, spans, order):
    count = lax.axis_size("seq")
    live = sorted(range(len(parts)), key=lambda index: -spans[index])
    sizes = [part.shape[0] for part in parts]
    state = jnp.concatenate([parts[index] for index in live], axis=0)[None]
    finished = {}
    for offset in order + [None]:
        while live and spans[live[-1]] <= state.shape[0]:
            index = live.pop()
            start = sum(sizes[other] for other in live)
            finished[index] = state[:, start : start + sizes[index]]
            state = state[:, :start]
        if not live:
            break
        moved = lax.ppermute(state, "seq", [(source, source ^ offset) for source in range(count)])
        state = jnp.concatenate([state, moved], axis=0)
    return [finished[index] for index in range(len(parts))]


def split_exact(value):
    high = lax.reduce_precision(value, exponent_bits=8, mantissa_bits=7)
    rest = value - high
    middle = lax.reduce_precision(rest, exponent_bits=8, mantissa_bits=7)
    low = rest - middle
    return jnp.stack([high, middle, low], axis=-1).astype(jnp.bfloat16)


def join_exact(parts):
    parts = parts.astype(jnp.float32)
    return (parts[..., 0] + parts[..., 1]) + parts[..., 2]


def stats_rows(rows, heads_dev):
    return -(-(rows * heads_dev * 6) // (16 * lane)) * 16


def pack_stats(lse_sel, delta_sel):
    rows, heads_dev = lse_sel.shape
    coded = split_exact(jnp.stack([lse_sel, delta_sel], axis=-1)).reshape(-1)
    padded = stats_rows(rows, heads_dev) * lane
    coded = jnp.pad(coded, (0, padded - coded.shape[0]))
    return coded.reshape(padded // lane, lane)


def unpack_stats(coded, slots, rows, heads_dev):
    flat = coded.reshape(slots, -1)[:, : rows * heads_dev * 6]
    values = join_exact(flat.reshape(slots * rows, heads_dev, 2, 3))
    return values[:, :, 0], values[:, :, 1]


def shards(query_rows, key_rows, value_rows, cotangent, norm_gain, offsets):
    tok_dev, heads_dev, head_size = query_rows.shape
    seq_count = lax.axis_size("seq")
    device = lax.axis_index("seq")
    group_rows = tok_dev * seq_count // RATE4
    score_scale = head_size ** (-0.5)
    features = heads_dev * head_size * lax.axis_size("head")

    levels = []
    for stride in RATES:
        span = max(1, stride * group_rows // tok_dev)
        rows = tok_dev // stride
        wanted = offsets % stride
        levels.append(
            dict(
                stride=stride,
                span=span,
                rows=rows,
                wanted=wanted,
                spot=device % span,
                key_sel=pick_rows(key_rows, wanted, stride),
                value_sel=pick_rows(value_rows, wanted, stride),
                query_sel=pick_rows(query_rows, wanted, stride),
            )
        )
    spans = [level["span"] for level in levels]
    order = exchange_order(seq_count)
    for level in levels:
        level["owner"] = level["spot"] ^ jnp.asarray(spread(order, level["span"]))

    key_sets = extend(
        [
            jnp.concatenate(
                [
                    level["key_sel"].reshape(-1, lane),
                    level["value_sel"].reshape(-1, lane),
                ],
                axis=0,
            )
            for level in levels
        ],
        spans,
        order,
    )
    query_sets = extend([level["query_sel"].reshape(-1, lane) for level in levels], spans, order)

    lse_total = jnp.full((tok_dev, heads_dev), neg_fill, jnp.float32)
    for level, key_set in zip(levels, key_sets):
        span, rows = level["span"], level["rows"]
        paired = key_set.reshape(span, 2, rows, heads_dev, head_size)
        keys = paired[:, 0].reshape(span * rows, heads_dev, head_size)
        level["key_all"] = keys
        level["value_all"] = paired[:, 1].reshape(span * rows, heads_dev, head_size)
        raw = (
            jnp.einsum("qhd,khd->hqk", level["query_sel"], keys, preferred_element_type=jnp.float32)
            * score_scale
        )
        key_at = (
            level["owner"][:, None] * rows + jnp.arange(rows, dtype=jnp.int32)[None, :]
        ).reshape(1, span * rows)
        query_at = (level["spot"] * rows + jnp.arange(rows, dtype=jnp.int32))[:, None]
        linked = key_at <= query_at
        scores = jnp.where(linked[None], raw, neg_fill)
        row_peak = jnp.max(scores, axis=2)
        level_lse = row_peak + jnp.log(jnp.sum(jnp.exp(scores - row_peak[:, :, None]), axis=2))
        level["scores"] = scores
        lse_total = jnp.logaddexp(
            lse_total, put_rows(level_lse.T, level["wanted"], level["stride"], neg_fill)
        )

    attended = jnp.zeros((tok_dev, heads_dev, head_size), jnp.float32)
    for level in levels:
        lse_sel = pick_rows(lse_total, level["wanted"], level["stride"])
        weights = jnp.exp(level["scores"] - lse_sel.T[:, :, None])
        level["lse_sel"] = lse_sel
        level["weights"] = weights
        out_sel = jnp.einsum(
            "hqk,khd->qhd", weights.astype(jnp.bfloat16), level["value_all"],
            preferred_element_type=jnp.float32,
        )
        attended = attended + put_rows(out_sel, level["wanted"], level["stride"], 0.0)

    grad_in = cotangent.astype(jnp.float32) * norm_gain[None]
    sums = lax.psum(
        jnp.stack(
            [
                jnp.sum(attended, axis=(1, 2)),
                jnp.sum(attended * attended, axis=(1, 2)),
                jnp.sum(grad_in, axis=(1, 2)),
                jnp.sum(grad_in * attended, axis=(1, 2)),
            ]
        ),
        "head",
    )
    centre = sums[0] / features
    variance = sums[1] / features - centre * centre
    inverse = lax.rsqrt(variance + epsilon)
    first_mean = sums[2] / features
    second_mean = inverse * (sums[3] / features - centre * first_mean)
    normed = (attended - centre[:, None, None]) * inverse[:, None, None]
    d_attended = (
        inverse[:, None, None]
        * (grad_in - first_mean[:, None, None] - normed * second_mean[:, None, None])
    ).astype(jnp.bfloat16)
    row_delta = jnp.sum(d_attended.astype(jnp.float32) * attended, axis=2)

    query_grad = jnp.zeros((tok_dev, heads_dev, head_size), jnp.float32)
    back_sets = []
    for level in levels:
        dout_sel = pick_rows(d_attended, level["wanted"], level["stride"])
        delta_sel = pick_rows(row_delta, level["wanted"], level["stride"])
        back_sets.append(
            jnp.concatenate(
                [dout_sel.reshape(-1, lane), pack_stats(level["lse_sel"], delta_sel)], axis=0
            )
        )
        weight_grad = jnp.einsum(
            "qhd,khd->hqk", dout_sel, level["value_all"], preferred_element_type=jnp.float32
        )
        score_grad = (level["weights"] * (weight_grad - delta_sel.T[:, :, None])).astype(
            jnp.bfloat16
        )
        grad_sel = jnp.einsum(
            "hqk,khd->qhd", score_grad, level["key_all"], preferred_element_type=jnp.float32
        )
        query_grad = query_grad + put_rows(
            grad_sel * score_scale, level["wanted"], level["stride"], 0.0
        )
    back_sets = extend(back_sets, spans, order)

    key_grad = jnp.zeros((tok_dev, heads_dev, head_size), jnp.float32)
    value_grad = jnp.zeros((tok_dev, heads_dev, head_size), jnp.float32)
    for level, query_set, back_set in zip(levels, query_sets, back_sets):
        span, rows = level["span"], level["rows"]
        queries = query_set.reshape(span * rows, heads_dev, head_size)
        back_slots = back_set.reshape(span, -1, lane)
        dout_all = back_slots[:, : rows * heads_dev].reshape(span * rows, heads_dev, head_size)
        lse_all, delta_all = unpack_stats(
            back_slots[:, rows * heads_dev :], span, rows, heads_dev
        )
        raw = (
            jnp.einsum(
                "qhd,khd->hqk", queries, level["key_sel"], preferred_element_type=jnp.float32
            )
            * score_scale
        )
        query_at = (
            level["owner"][:, None] * rows + jnp.arange(rows, dtype=jnp.int32)[None, :]
        ).reshape(span * rows, 1)
        key_at = (level["spot"] * rows + jnp.arange(rows, dtype=jnp.int32))[None, :]
        linked = query_at >= key_at
        scores = jnp.where(linked[None], raw, neg_fill)
        weights = jnp.exp(scores - lse_all.T[:, :, None])
        value_grad_sel = jnp.einsum(
            "hqk,qhd->khd", weights.astype(jnp.bfloat16), dout_all,
            preferred_element_type=jnp.float32,
        )
        weight_grad = jnp.einsum(
            "qhd,khd->hqk", dout_all, level["value_sel"], preferred_element_type=jnp.float32
        )
        score_grad = (weights * (weight_grad - delta_all.T[:, :, None])).astype(jnp.bfloat16)
        key_grad_sel = jnp.einsum(
            "hqk,qhd->khd", score_grad, queries, preferred_element_type=jnp.float32
        )
        key_grad = key_grad + put_rows(
            key_grad_sel * score_scale, level["wanted"], level["stride"], 0.0
        )
        value_grad = value_grad + put_rows(value_grad_sel, level["wanted"], level["stride"], 0.0)

    return (
        query_grad.astype(jnp.bfloat16),
        key_grad.astype(jnp.bfloat16),
        value_grad.astype(jnp.bfloat16),
    )


def solution(mesh):
    placed = (
        P("seq", "head", None),
        P("seq", "head", None),
        P("seq", "head", None),
        P("seq", "head", None),
        P("head", None),
        P("head"),
    )
    return jax.shard_map(
        shards,
        mesh=mesh,
        in_specs=placed,
        out_specs=(P("seq", "head", None), P("seq", "head", None), P("seq", "head", None)),
        check_vma=False,
    )
```

```python
import numpy as np
import jax
import jax.numpy as jnp
from jax import lax
from jax.sharding import PartitionSpec as P

RATE2 = 4
RATE3 = 16
RATE4 = 32
RATES = (1, RATE2, RATE3, RATE4)

neg_fill = -1e30
epsilon = 1e-05
lane = 128


def pick_rows(source, wanted, stride):
    row_count = source.shape[0] // stride
    shaped = source.reshape((row_count, stride) + source.shape[1:])
    trailing = (1,) * (source.ndim - 2)
    target = wanted.reshape((1, 1, -1) + trailing)
    column = jnp.arange(stride, dtype=jnp.int32).reshape((1, stride, 1) + trailing)
    zeroed = jnp.where(column == target, shaped, jnp.zeros((), source.dtype))
    return jnp.sum(zeroed, axis=1, dtype=source.dtype)


def put_rows(compact, wanted, stride, filler):
    trailing = (1,) * (compact.ndim - 2)
    target = wanted.reshape((1, 1, -1) + trailing)
    column = jnp.arange(stride, dtype=jnp.int32).reshape((1, stride, 1) + trailing)
    spread = jnp.where(column == target, compact[:, None], jnp.asarray(filler, compact.dtype))
    return spread.reshape((compact.shape[0] * stride,) + compact.shape[1:])


def exchange_order(count):
    bits = [1 << bit for bit in range(max(0, (count - 1).bit_length()))]
    order = []
    for first in range(0, len(bits), 2):
        order.extend(reversed(bits[first : first + 2]))
    return order


def spread(order, slots):
    table = np.zeros(slots, np.int32)
    for slot in range(slots):
        for bit, offset in enumerate(order):
            if slot >> bit & 1:
                table[slot] ^= offset
    return table


def extend(parts, spans, order):
    count = lax.axis_size("seq")
    live = sorted(range(len(parts)), key=lambda index: -spans[index])
    sizes = [part.shape[0] for part in parts]
    state = jnp.concatenate([parts[index] for index in live], axis=0)[None]
    finished = {}
    for offset in order + [None]:
        while live and spans[live[-1]] <= state.shape[0]:
            index = live.pop()
            start = sum(sizes[other] for other in live)
            finished[index] = state[:, start : start + sizes[index]]
            state = state[:, :start]
        if not live:
            break
        moved = lax.ppermute(state, "seq", [(source, source ^ offset) for source in range(count)])
        state = jnp.concatenate([state, moved], axis=0)
    return [finished[index] for index in range(len(parts))]


def split_exact(value):
    high = lax.reduce_precision(value, exponent_bits=8, mantissa_bits=7)
    rest = value - high
    middle = lax.reduce_precision(rest, exponent_bits=8, mantissa_bits=7)
    low = rest - middle
    return jnp.stack([high, middle, low]).astype(jnp.bfloat16)


def stats_rows(rows, heads_dev):
    return -(-(rows * heads_dev * 6) // (16 * lane)) * 16


def pack_stats(lse_sel, delta_sel):
    rows, heads_dev = lse_sel.shape
    coded = split_exact(jnp.stack([lse_sel.T, delta_sel.T])).reshape(-1)
    padded = stats_rows(rows, heads_dev) * lane
    coded = jnp.pad(coded, (0, padded - coded.shape[0]))
    return coded.reshape(padded // lane, lane)


def unpack_stats(coded, slots, rows, heads_dev):
    width = 2 * heads_dev * rows
    parts = coded.reshape(slots, -1)[:, : 3 * width].reshape(slots, 3, width)
    parts = parts.astype(jnp.float32)
    values = (parts[:, 0] + parts[:, 1]) + parts[:, 2]
    values = values.reshape(slots, 2, heads_dev, rows).transpose(1, 2, 0, 3)
    values = values.reshape(2, heads_dev, slots * rows)
    return values[0], values[1]


def shards(query_rows, key_rows, value_rows, cotangent, norm_gain, offsets):
    tok_dev, heads_dev, head_size = query_rows.shape
    seq_count = lax.axis_size("seq")
    device = lax.axis_index("seq")
    group_rows = tok_dev * seq_count // RATE4
    score_scale = head_size ** (-0.5)
    features = heads_dev * head_size * lax.axis_size("head")

    levels = []
    for stride in RATES:
        span = max(1, stride * group_rows // tok_dev)
        rows = tok_dev // stride
        wanted = offsets % stride
        levels.append(
            dict(
                stride=stride,
                span=span,
                rows=rows,
                wanted=wanted,
                spot=device % span,
                key_sel=pick_rows(key_rows, wanted, stride),
                value_sel=pick_rows(value_rows, wanted, stride),
                query_sel=pick_rows(query_rows, wanted, stride),
            )
        )
    spans = [level["span"] for level in levels]
    order = exchange_order(seq_count)
    for level in levels:
        level["owner"] = level["spot"] ^ jnp.asarray(spread(order, level["span"]))

    key_sets = extend(
        [
            jnp.concatenate(
                [
                    level["key_sel"].reshape(-1, lane),
                    level["value_sel"].reshape(-1, lane),
                ],
                axis=0,
            )
            for level in levels
        ],
        spans,
        order,
    )
    query_sets = extend([level["query_sel"].reshape(-1, lane) for level in levels], spans, order)

    lse_total = jnp.full((tok_dev, heads_dev), neg_fill, jnp.float32)
    for level, key_set in zip(levels, key_sets):
        span, rows = level["span"], level["rows"]
        paired = key_set.reshape(span, 2, rows, heads_dev, head_size)
        keys = paired[:, 0].reshape(span * rows, heads_dev, head_size)
        level["key_all"] = keys
        level["value_all"] = paired[:, 1].reshape(span * rows, heads_dev, head_size)
        raw = (
            jnp.einsum("qhd,khd->hqk", level["query_sel"], keys, preferred_element_type=jnp.float32)
            * score_scale
        )
        key_at = (
            level["owner"][:, None] * rows + jnp.arange(rows, dtype=jnp.int32)[None, :]
        ).reshape(1, span * rows)
        query_at = (level["spot"] * rows + jnp.arange(rows, dtype=jnp.int32))[:, None]
        linked = key_at <= query_at
        scores = jnp.where(linked[None], raw, neg_fill)
        row_peak = jnp.max(scores, axis=2)
        level_lse = row_peak + jnp.log(jnp.sum(jnp.exp(scores - row_peak[:, :, None]), axis=2))
        level["scores"] = scores
        lse_total = jnp.logaddexp(
            lse_total, put_rows(level_lse.T, level["wanted"], level["stride"], neg_fill)
        )

    attended = jnp.zeros((tok_dev, heads_dev, head_size), jnp.float32)
    for level in levels:
        lse_sel = pick_rows(lse_total, level["wanted"], level["stride"])
        weights = jnp.exp(level["scores"] - lse_sel.T[:, :, None])
        level["lse_sel"] = lse_sel
        level["weights"] = weights
        out_sel = jnp.einsum(
            "hqk,khd->qhd", weights.astype(jnp.bfloat16), level["value_all"],
            preferred_element_type=jnp.float32,
        )
        attended = attended + put_rows(out_sel, level["wanted"], level["stride"], 0.0)

    grad_in = cotangent.astype(jnp.float32) * norm_gain[None]
    sums = lax.psum(
        jnp.stack(
            [
                jnp.sum(attended, axis=(1, 2)),
                jnp.sum(attended * attended, axis=(1, 2)),
                jnp.sum(grad_in, axis=(1, 2)),
                jnp.sum(grad_in * attended, axis=(1, 2)),
            ]
        ),
        "head",
    )
    centre = sums[0] / features
    variance = sums[1] / features - centre * centre
    inverse = lax.rsqrt(variance + epsilon)
    first_mean = sums[2] / features
    second_mean = inverse * (sums[3] / features - centre * first_mean)
    normed = (attended - centre[:, None, None]) * inverse[:, None, None]
    d_attended = (
        inverse[:, None, None]
        * (grad_in - first_mean[:, None, None] - normed * second_mean[:, None, None])
    ).astype(jnp.bfloat16)
    row_delta = jnp.sum(d_attended.astype(jnp.float32) * attended, axis=2)

    query_grad = jnp.zeros((tok_dev, heads_dev, head_size), jnp.float32)
    back_sets = []
    for level in levels:
        dout_sel = pick_rows(d_attended, level["wanted"], level["stride"])
        delta_sel = pick_rows(row_delta, level["wanted"], level["stride"])
        back_sets.append(
            jnp.concatenate(
                [dout_sel.reshape(-1, lane), pack_stats(level["lse_sel"], delta_sel)], axis=0
            )
        )
        weight_grad = jnp.einsum(
            "qhd,khd->hqk", dout_sel, level["value_all"], preferred_element_type=jnp.float32
        )
        score_grad = (level["weights"] * (weight_grad - delta_sel.T[:, :, None])).astype(
            jnp.bfloat16
        )
        grad_sel = jnp.einsum(
            "hqk,khd->qhd", score_grad, level["key_all"], preferred_element_type=jnp.float32
        )
        query_grad = query_grad + put_rows(
            grad_sel * score_scale, level["wanted"], level["stride"], 0.0
        )
    back_sets = extend(back_sets, spans, order)

    key_grad = jnp.zeros((tok_dev, heads_dev, head_size), jnp.float32)
    value_grad = jnp.zeros((tok_dev, heads_dev, head_size), jnp.float32)
    for level, query_set, back_set in zip(levels, query_sets, back_sets):
        span, rows = level["span"], level["rows"]
        queries = query_set.reshape(span * rows, heads_dev, head_size)
        back_slots = back_set.reshape(span, -1, lane)
        dout_all = back_slots[:, : rows * heads_dev].reshape(span * rows, heads_dev, head_size)
        lse_all, delta_all = unpack_stats(
            back_slots[:, rows * heads_dev :], span, rows, heads_dev
        )
        raw = (
            jnp.einsum(
                "qhd,khd->hqk", queries, level["key_sel"], preferred_element_type=jnp.float32
            )
            * score_scale
        )
        query_at = (
            level["owner"][:, None] * rows + jnp.arange(rows, dtype=jnp.int32)[None, :]
        ).reshape(span * rows, 1)
        key_at = (level["spot"] * rows + jnp.arange(rows, dtype=jnp.int32))[None, :]
        linked = query_at >= key_at
        scores = jnp.where(linked[None], raw, neg_fill)
        weights = jnp.exp(scores - lse_all[:, :, None])
        value_grad_sel = jnp.einsum(
            "hqk,qhd->khd", weights.astype(jnp.bfloat16), dout_all,
            preferred_element_type=jnp.float32,
        )
        weight_grad = jnp.einsum(
            "qhd,khd->hqk", dout_all, level["value_sel"], preferred_element_type=jnp.float32
        )
        score_grad = (weights * (weight_grad - delta_all[:, :, None])).astype(jnp.bfloat16)
        key_grad_sel = jnp.einsum(
            "hqk,qhd->khd", score_grad, queries, preferred_element_type=jnp.float32
        )
        key_grad = key_grad + put_rows(
            key_grad_sel * score_scale, level["wanted"], level["stride"], 0.0
        )
        value_grad = value_grad + put_rows(value_grad_sel, level["wanted"], level["stride"], 0.0)

    return (
        query_grad.astype(jnp.bfloat16),
        key_grad.astype(jnp.bfloat16),
        value_grad.astype(jnp.bfloat16),
    )


def solution(mesh):
    placed = (
        P("seq", "head", None),
        P("seq", "head", None),
        P("seq", "head", None),
        P("seq", "head", None),
        P("head", None),
        P("head"),
    )
    return jax.shard_map(
        shards,
        mesh=mesh,
        in_specs=placed,
        out_specs=(P("seq", "head", None), P("seq", "head", None), P("seq", "head", None)),
        check_vma=False,
    )
```

```python
import numpy as np
import jax
import jax.numpy as jnp
from jax import lax
from jax.sharding import PartitionSpec as P

RATE2 = 4
RATE3 = 16
RATE4 = 32
RATES = (1, RATE2, RATE3, RATE4)

neg_fill = -1e30
epsilon = 1e-05
lane = 128


def pick_rows(source, wanted, stride):
    row_count = source.shape[0] // stride
    shaped = source.reshape((row_count, stride) + source.shape[1:])
    trailing = (1,) * (source.ndim - 2)
    target = wanted.reshape((1, 1, -1) + trailing)
    column = jnp.arange(stride, dtype=jnp.int32).reshape((1, stride, 1) + trailing)
    zeroed = jnp.where(column == target, shaped, jnp.zeros((), source.dtype))
    return jnp.sum(zeroed, axis=1, dtype=source.dtype)


def put_rows(compact, wanted, stride, filler):
    trailing = (1,) * (compact.ndim - 2)
    target = wanted.reshape((1, 1, -1) + trailing)
    column = jnp.arange(stride, dtype=jnp.int32).reshape((1, stride, 1) + trailing)
    spread = jnp.where(column == target, compact[:, None], jnp.asarray(filler, compact.dtype))
    return spread.reshape((compact.shape[0] * stride,) + compact.shape[1:])


def exchange_order(count):
    bits = [1 << bit for bit in range(max(0, (count - 1).bit_length()))]
    order = []
    for first in range(0, len(bits), 2):
        order.extend(reversed(bits[first : first + 2]))
    return order


def spread(order, slots):
    table = np.zeros(slots, np.int32)
    for slot in range(slots):
        for bit, offset in enumerate(order):
            if slot >> bit & 1:
                table[slot] ^= offset
    return table


def extend(parts, spans, order):
    count = lax.axis_size("seq")
    live = sorted(range(len(parts)), key=lambda index: -spans[index])
    sizes = [part.shape[0] for part in parts]
    state = jnp.concatenate([parts[index] for index in live], axis=0)[None]
    finished = {}
    for offset in order + [None]:
        while live and spans[live[-1]] <= state.shape[0]:
            index = live.pop()
            start = sum(sizes[other] for other in live)
            finished[index] = state[:, start : start + sizes[index]]
            state = state[:, :start]
        if not live:
            break
        moved = lax.ppermute(state, "seq", [(source, source ^ offset) for source in range(count)])
        state = jnp.concatenate([state, moved], axis=0)
    return [finished[index] for index in range(len(parts))]


def split_exact(value):
    high = lax.reduce_precision(value, exponent_bits=8, mantissa_bits=7)
    rest = value - high
    middle = lax.reduce_precision(rest, exponent_bits=8, mantissa_bits=7)
    low = rest - middle
    return jnp.stack([high, middle, low]).astype(jnp.bfloat16)


def stats_rows(rows, heads_dev):
    return -(-(rows * heads_dev * 6) // (16 * lane)) * 16


def pack_stats(lse_sel, delta_sel):
    rows, heads_dev = lse_sel.shape
    coded = split_exact(jnp.stack([lse_sel.T, delta_sel.T])).reshape(-1)
    padded = stats_rows(rows, heads_dev) * lane
    coded = jnp.pad(coded, (0, padded - coded.shape[0]))
    return coded.reshape(padded // lane, lane)


def unpack_stats(coded, slots, rows, heads_dev):
    width = 2 * heads_dev * rows
    parts = coded.reshape(slots, -1)[:, : 3 * width].reshape(slots, 3, width)
    parts = parts.astype(jnp.float32)
    values = (parts[:, 0] + parts[:, 1]) + parts[:, 2]
    values = values.reshape(slots, 2, heads_dev, rows).transpose(1, 2, 0, 3)
    values = values.reshape(2, heads_dev, slots * rows)
    return values[0], values[1]


def shards(query_rows, key_rows, value_rows, cotangent, norm_gain, offsets):
    tok_dev, heads_dev, head_size = query_rows.shape
    seq_count = lax.axis_size("seq")
    device = lax.axis_index("seq")
    group_rows = tok_dev * seq_count // RATE4
    score_scale = head_size ** (-0.5)
    features = heads_dev * head_size * lax.axis_size("head")

    levels = []
    for stride in RATES:
        span = max(1, stride * group_rows // tok_dev)
        rows = tok_dev // stride
        wanted = offsets % stride
        levels.append(
            dict(
                stride=stride,
                span=span,
                rows=rows,
                wanted=wanted,
                spot=device % span,
                key_sel=pick_rows(key_rows, wanted, stride),
                value_sel=pick_rows(value_rows, wanted, stride),
                query_sel=pick_rows(query_rows, wanted, stride),
            )
        )
    spans = [level["span"] for level in levels]
    order = exchange_order(seq_count)
    for level in levels:
        level["owner"] = level["spot"] ^ jnp.asarray(spread(order, level["span"]))

    key_sets = extend(
        [
            jnp.concatenate(
                [
                    level["key_sel"].reshape(-1, lane),
                    level["value_sel"].reshape(-1, lane),
                ],
                axis=0,
            )
            for level in levels
        ],
        spans,
        order,
    )
    query_parts, key_sets = lax.optimization_barrier(
        ([level["query_sel"].reshape(-1, lane) for level in levels], key_sets)
    )
    query_sets = extend(query_parts, spans, order)

    lse_total = jnp.full((tok_dev, heads_dev), neg_fill, jnp.float32)
    for level, key_set in zip(levels, key_sets):
        span, rows = level["span"], level["rows"]
        paired = key_set.reshape(span, 2, rows, heads_dev, head_size)
        keys = paired[:, 0].reshape(span * rows, heads_dev, head_size)
        level["key_all"] = keys
        level["value_all"] = paired[:, 1].reshape(span * rows, heads_dev, head_size)
        raw = (
            jnp.einsum("qhd,khd->hqk", level["query_sel"], keys, preferred_element_type=jnp.float32)
            * score_scale
        )
        key_at = (
            level["owner"][:, None] * rows + jnp.arange(rows, dtype=jnp.int32)[None, :]
        ).reshape(1, span * rows)
        query_at = (level["spot"] * rows + jnp.arange(rows, dtype=jnp.int32))[:, None]
        linked = key_at <= query_at
        scores = jnp.where(linked[None], raw, neg_fill)
        row_peak = jnp.max(scores, axis=2)
        level_lse = row_peak + jnp.log(jnp.sum(jnp.exp(scores - row_peak[:, :, None]), axis=2))
        level["scores"] = scores
        lse_total = jnp.logaddexp(
            lse_total, put_rows(level_lse.T, level["wanted"], level["stride"], neg_fill)
        )

    attended = jnp.zeros((tok_dev, heads_dev, head_size), jnp.float32)
    for level in levels:
        lse_sel = pick_rows(lse_total, level["wanted"], level["stride"])
        weights = jnp.exp(level["scores"] - lse_sel.T[:, :, None])
        level["lse_sel"] = lse_sel
        level["weights"] = weights
        out_sel = jnp.einsum(
            "hqk,khd->qhd", weights.astype(jnp.bfloat16), level["value_all"],
            preferred_element_type=jnp.float32,
        )
        attended = attended + put_rows(out_sel, level["wanted"], level["stride"], 0.0)

    grad_in = cotangent.astype(jnp.float32) * norm_gain[None]
    sums = lax.psum(
        jnp.stack(
            [
                jnp.sum(attended, axis=(1, 2)),
                jnp.sum(attended * attended, axis=(1, 2)),
                jnp.sum(grad_in, axis=(1, 2)),
                jnp.sum(grad_in * attended, axis=(1, 2)),
            ]
        ),
        "head",
    )
    centre = sums[0] / features
    variance = sums[1] / features - centre * centre
    inverse = lax.rsqrt(variance + epsilon)
    first_mean = sums[2] / features
    second_mean = inverse * (sums[3] / features - centre * first_mean)
    normed = (attended - centre[:, None, None]) * inverse[:, None, None]
    d_attended = (
        inverse[:, None, None]
        * (grad_in - first_mean[:, None, None] - normed * second_mean[:, None, None])
    ).astype(jnp.bfloat16)
    row_delta = jnp.sum(d_attended.astype(jnp.float32) * attended, axis=2)

    query_grad = jnp.zeros((tok_dev, heads_dev, head_size), jnp.float32)
    back_sets = []
    for level in levels:
        dout_sel = pick_rows(d_attended, level["wanted"], level["stride"])
        delta_sel = pick_rows(row_delta, level["wanted"], level["stride"])
        back_sets.append(
            jnp.concatenate(
                [dout_sel.reshape(-1, lane), pack_stats(level["lse_sel"], delta_sel)], axis=0
            )
        )
        weight_grad = jnp.einsum(
            "qhd,khd->hqk", dout_sel, level["value_all"], preferred_element_type=jnp.float32
        )
        score_grad = (level["weights"] * (weight_grad - delta_sel.T[:, :, None])).astype(
            jnp.bfloat16
        )
        grad_sel = jnp.einsum(
            "hqk,khd->qhd", score_grad, level["key_all"], preferred_element_type=jnp.float32
        )
        query_grad = query_grad + put_rows(
            grad_sel * score_scale, level["wanted"], level["stride"], 0.0
        )
    back_sets, query_sets = lax.optimization_barrier((back_sets, query_sets))
    back_sets = extend(back_sets, spans, order)

    key_grad = jnp.zeros((tok_dev, heads_dev, head_size), jnp.float32)
    value_grad = jnp.zeros((tok_dev, heads_dev, head_size), jnp.float32)
    for level, query_set, back_set in zip(levels, query_sets, back_sets):
        span, rows = level["span"], level["rows"]
        queries = query_set.reshape(span * rows, heads_dev, head_size)
        back_slots = back_set.reshape(span, -1, lane)
        dout_all = back_slots[:, : rows * heads_dev].reshape(span * rows, heads_dev, head_size)
        lse_all, delta_all = unpack_stats(
            back_slots[:, rows * heads_dev :], span, rows, heads_dev
        )
        raw = (
            jnp.einsum(
                "qhd,khd->hqk", queries, level["key_sel"], preferred_element_type=jnp.float32
            )
            * score_scale
        )
        query_at = (
            level["owner"][:, None] * rows + jnp.arange(rows, dtype=jnp.int32)[None, :]
        ).reshape(span * rows, 1)
        key_at = (level["spot"] * rows + jnp.arange(rows, dtype=jnp.int32))[None, :]
        linked = query_at >= key_at
        scores = jnp.where(linked[None], raw, neg_fill)
        weights = jnp.exp(scores - lse_all[:, :, None])
        value_grad_sel = jnp.einsum(
            "hqk,qhd->khd", weights.astype(jnp.bfloat16), dout_all,
            preferred_element_type=jnp.float32,
        )
        weight_grad = jnp.einsum(
            "qhd,khd->hqk", dout_all, level["value_sel"], preferred_element_type=jnp.float32
        )
        score_grad = (weights * (weight_grad - delta_all[:, :, None])).astype(jnp.bfloat16)
        key_grad_sel = jnp.einsum(
            "hqk,qhd->khd", score_grad, queries, preferred_element_type=jnp.float32
        )
        key_grad = key_grad + put_rows(
            key_grad_sel * score_scale, level["wanted"], level["stride"], 0.0
        )
        value_grad = value_grad + put_rows(value_grad_sel, level["wanted"], level["stride"], 0.0)

    return (
        query_grad.astype(jnp.bfloat16),
        key_grad.astype(jnp.bfloat16),
        value_grad.astype(jnp.bfloat16),
    )


def solution(mesh):
    placed = (
        P("seq", "head", None),
        P("seq", "head", None),
        P("seq", "head", None),
        P("seq", "head", None),
        P("head", None),
        P("head"),
    )
    return jax.shard_map(
        shards,
        mesh=mesh,
        in_specs=placed,
        out_specs=(P("seq", "head", None), P("seq", "head", None), P("seq", "head", None)),
        check_vma=False,
    )
```

```python
import numpy as np
import jax
import jax.numpy as jnp
from jax import lax
from jax.sharding import PartitionSpec as P

RATE2 = 4
RATE3 = 16
RATE4 = 32
RATES = (1, RATE2, RATE3, RATE4)

neg_fill = -1e30
epsilon = 1e-05
lane = 128


def pick_rows(source, wanted, stride):
    row_count = source.shape[0] // stride
    shaped = source.reshape((row_count, stride) + source.shape[1:])
    trailing = (1,) * (source.ndim - 2)
    target = wanted.reshape((1, 1, -1) + trailing)
    column = jnp.arange(stride, dtype=jnp.int32).reshape((1, stride, 1) + trailing)
    zeroed = jnp.where(column == target, shaped, jnp.zeros((), source.dtype))
    return jnp.sum(zeroed, axis=1, dtype=source.dtype)


def put_rows(compact, wanted, stride, filler):
    trailing = (1,) * (compact.ndim - 2)
    target = wanted.reshape((1, 1, -1) + trailing)
    column = jnp.arange(stride, dtype=jnp.int32).reshape((1, stride, 1) + trailing)
    spread = jnp.where(column == target, compact[:, None], jnp.asarray(filler, compact.dtype))
    return spread.reshape((compact.shape[0] * stride,) + compact.shape[1:])


def exchange_order(count):
    bits = [1 << bit for bit in range(max(0, (count - 1).bit_length()))]
    order = []
    for first in range(0, len(bits), 2):
        order.extend(reversed(bits[first : first + 2]))
    return order


def spread(order, slots):
    table = np.zeros(slots, np.int32)
    for slot in range(slots):
        for bit, offset in enumerate(order):
            if slot >> bit & 1:
                table[slot] ^= offset
    return table


def extend(parts, spans, order):
    count = lax.axis_size("seq")
    live = sorted(range(len(parts)), key=lambda index: -spans[index])
    sizes = [part.shape[0] for part in parts]
    state = jnp.concatenate([parts[index] for index in live], axis=0)[None]
    finished = {}
    for offset in order + [None]:
        while live and spans[live[-1]] <= state.shape[0]:
            index = live.pop()
            start = sum(sizes[other] for other in live)
            finished[index] = state[:, start : start + sizes[index]]
            state = state[:, :start]
        if not live:
            break
        moved = lax.ppermute(state, "seq", [(source, source ^ offset) for source in range(count)])
        state = jnp.concatenate([state, moved], axis=0)
    return [finished[index] for index in range(len(parts))]


def split_exact(value):
    high = lax.reduce_precision(value, exponent_bits=8, mantissa_bits=7)
    rest = value - high
    middle = lax.reduce_precision(rest, exponent_bits=8, mantissa_bits=7)
    low = rest - middle
    return jnp.stack([high, middle, low]).astype(jnp.bfloat16)


def stats_rows(rows, heads_dev):
    return -(-(rows * heads_dev * 6) // (16 * lane)) * 16


def pack_stats(lse_sel, delta_sel):
    rows, heads_dev = lse_sel.shape
    coded = split_exact(jnp.stack([lse_sel.T, delta_sel.T])).reshape(-1)
    padded = stats_rows(rows, heads_dev) * lane
    coded = jnp.pad(coded, (0, padded - coded.shape[0]))
    return coded.reshape(padded // lane, lane)


def unpack_stats(coded, slots, rows, heads_dev):
    width = 2 * heads_dev * rows
    parts = coded.reshape(slots, -1)[:, : 3 * width].reshape(slots, 3, width)
    parts = parts.astype(jnp.float32)
    values = (parts[:, 0] + parts[:, 1]) + parts[:, 2]
    values = values.reshape(slots, 2, heads_dev, rows).transpose(1, 2, 0, 3)
    values = values.reshape(2, heads_dev, slots * rows)
    return values[0], values[1]


def shards(query_rows, key_rows, value_rows, cotangent, norm_gain, offsets):
    tok_dev, heads_dev, head_size = query_rows.shape
    seq_count = lax.axis_size("seq")
    device = lax.axis_index("seq")
    group_rows = tok_dev * seq_count // RATE4
    score_scale = head_size ** (-0.5)
    features = heads_dev * head_size * lax.axis_size("head")

    levels = []
    for stride in RATES:
        span = max(1, stride * group_rows // tok_dev)
        rows = tok_dev // stride
        wanted = offsets % stride
        levels.append(
            dict(
                stride=stride,
                span=span,
                rows=rows,
                wanted=wanted,
                spot=device % span,
                key_sel=pick_rows(key_rows, wanted, stride),
                value_sel=pick_rows(value_rows, wanted, stride),
                query_sel=pick_rows(query_rows, wanted, stride),
            )
        )
    spans = [level["span"] for level in levels]
    order = exchange_order(seq_count)
    for level in levels:
        level["owner"] = level["spot"] ^ jnp.asarray(spread(order, level["span"]))

    key_sets = extend([level["key_sel"].reshape(-1, lane) for level in levels], spans, order)
    value_sets = extend([level["value_sel"].reshape(-1, lane) for level in levels], spans, order)
    query_sets = extend([level["query_sel"].reshape(-1, lane) for level in levels], spans, order)

    lse_total = jnp.full((tok_dev, heads_dev), neg_fill, jnp.float32)
    for level, key_set, value_set in zip(levels, key_sets, value_sets):
        span, rows = level["span"], level["rows"]
        keys = key_set.reshape(span * rows, heads_dev, head_size)
        level["key_all"] = keys
        level["value_all"] = value_set.reshape(span * rows, heads_dev, head_size)
        raw = (
            jnp.einsum("qhd,khd->hqk", level["query_sel"], keys, preferred_element_type=jnp.float32)
            * score_scale
        )
        key_at = (
            level["owner"][:, None] * rows + jnp.arange(rows, dtype=jnp.int32)[None, :]
        ).reshape(1, span * rows)
        query_at = (level["spot"] * rows + jnp.arange(rows, dtype=jnp.int32))[:, None]
        linked = key_at <= query_at
        scores = jnp.where(linked[None], raw, neg_fill)
        row_peak = jnp.max(scores, axis=2)
        level_lse = row_peak + jnp.log(jnp.sum(jnp.exp(scores - row_peak[:, :, None]), axis=2))
        level["scores"] = scores
        lse_total = jnp.logaddexp(
            lse_total, put_rows(level_lse.T, level["wanted"], level["stride"], neg_fill)
        )

    attended = jnp.zeros((tok_dev, heads_dev, head_size), jnp.float32)
    for level in levels:
        lse_sel = pick_rows(lse_total, level["wanted"], level["stride"])
        weights = jnp.exp(level["scores"] - lse_sel.T[:, :, None])
        level["lse_sel"] = lse_sel
        level["weights"] = weights
        out_sel = jnp.einsum(
            "hqk,khd->qhd", weights.astype(jnp.bfloat16), level["value_all"],
            preferred_element_type=jnp.float32,
        )
        attended = attended + put_rows(out_sel, level["wanted"], level["stride"], 0.0)

    grad_in = cotangent.astype(jnp.float32) * norm_gain[None]
    sums = lax.psum(
        jnp.stack(
            [
                jnp.sum(attended, axis=(1, 2)),
                jnp.sum(attended * attended, axis=(1, 2)),
                jnp.sum(grad_in, axis=(1, 2)),
                jnp.sum(grad_in * attended, axis=(1, 2)),
            ]
        ),
        "head",
    )
    centre = sums[0] / features
    variance = sums[1] / features - centre * centre
    inverse = lax.rsqrt(variance + epsilon)
    first_mean = sums[2] / features
    second_mean = inverse * (sums[3] / features - centre * first_mean)
    normed = (attended - centre[:, None, None]) * inverse[:, None, None]
    d_attended = (
        inverse[:, None, None]
        * (grad_in - first_mean[:, None, None] - normed * second_mean[:, None, None])
    ).astype(jnp.bfloat16)
    row_delta = jnp.sum(d_attended.astype(jnp.float32) * attended, axis=2)

    query_grad = jnp.zeros((tok_dev, heads_dev, head_size), jnp.float32)
    back_sets = []
    other_sets = []
    for level in levels:
        dout_sel = pick_rows(d_attended, level["wanted"], level["stride"])
        delta_sel = pick_rows(row_delta, level["wanted"], level["stride"])
        back_sets.append(
            jnp.concatenate([dout_sel[:, 0], pack_stats(level["lse_sel"], delta_sel)], axis=0)
        )
        other_sets.append(dout_sel[:, 1:].reshape(-1, lane))
        weight_grad = jnp.einsum(
            "qhd,khd->hqk", dout_sel, level["value_all"], preferred_element_type=jnp.float32
        )
        score_grad = (level["weights"] * (weight_grad - delta_sel.T[:, :, None])).astype(
            jnp.bfloat16
        )
        grad_sel = jnp.einsum(
            "hqk,khd->qhd", score_grad, level["key_all"], preferred_element_type=jnp.float32
        )
        query_grad = query_grad + put_rows(
            grad_sel * score_scale, level["wanted"], level["stride"], 0.0
        )
    back_sets = extend(back_sets, spans, order)
    other_sets = extend(other_sets, spans, order)

    key_grad = jnp.zeros((tok_dev, heads_dev, head_size), jnp.float32)
    value_grad = jnp.zeros((tok_dev, heads_dev, head_size), jnp.float32)
    for level, query_set, back_set, other_set in zip(levels, query_sets, back_sets, other_sets):
        span, rows = level["span"], level["rows"]
        queries = query_set.reshape(span * rows, heads_dev, head_size)
        back_slots = back_set.reshape(span, -1, lane)
        dout_all = jnp.concatenate(
            [
                back_slots[:, :rows].reshape(span, rows, 1, head_size),
                other_set.reshape(span, rows, heads_dev - 1, head_size),
            ],
            axis=2,
        ).reshape(span * rows, heads_dev, head_size)
        lse_all, delta_all = unpack_stats(back_slots[:, rows:], span, rows, heads_dev)
        raw = (
            jnp.einsum(
                "qhd,khd->hqk", queries, level["key_sel"], preferred_element_type=jnp.float32
            )
            * score_scale
        )
        query_at = (
            level["owner"][:, None] * rows + jnp.arange(rows, dtype=jnp.int32)[None, :]
        ).reshape(span * rows, 1)
        key_at = (level["spot"] * rows + jnp.arange(rows, dtype=jnp.int32))[None, :]
        linked = query_at >= key_at
        scores = jnp.where(linked[None], raw, neg_fill)
        weights = jnp.exp(scores - lse_all[:, :, None])
        value_grad_sel = jnp.einsum(
            "hqk,qhd->khd", weights.astype(jnp.bfloat16), dout_all,
            preferred_element_type=jnp.float32,
        )
        weight_grad = jnp.einsum(
            "qhd,khd->hqk", dout_all, level["value_sel"], preferred_element_type=jnp.float32
        )
        score_grad = (weights * (weight_grad - delta_all[:, :, None])).astype(jnp.bfloat16)
        key_grad_sel = jnp.einsum(
            "hqk,qhd->khd", score_grad, queries, preferred_element_type=jnp.float32
        )
        key_grad = key_grad + put_rows(
            key_grad_sel * score_scale, level["wanted"], level["stride"], 0.0
        )
        value_grad = value_grad + put_rows(value_grad_sel, level["wanted"], level["stride"], 0.0)

    return (
        query_grad.astype(jnp.bfloat16),
        key_grad.astype(jnp.bfloat16),
        value_grad.astype(jnp.bfloat16),
    )


def solution(mesh):
    placed = (
        P("seq", "head", None),
        P("seq", "head", None),
        P("seq", "head", None),
        P("seq", "head", None),
        P("head", None),
        P("head"),
    )
    return jax.shard_map(
        shards,
        mesh=mesh,
        in_specs=placed,
        out_specs=(P("seq", "head", None), P("seq", "head", None), P("seq", "head", None)),
        check_vma=False,
    )
```

```python
import numpy as np
import jax
import jax.numpy as jnp
from jax import lax
from jax.sharding import PartitionSpec as P

RATE2 = 4
RATE3 = 16
RATE4 = 32
RATES = (1, RATE2, RATE3, RATE4)

neg_fill = -1e30
epsilon = 1e-05
lane = 128


def pick_rows(source, wanted, stride):
    row_count = source.shape[0] // stride
    shaped = source.reshape((row_count, stride) + source.shape[1:])
    trailing = (1,) * (source.ndim - 2)
    target = wanted.reshape((1, 1, -1) + trailing)
    column = jnp.arange(stride, dtype=jnp.int32).reshape((1, stride, 1) + trailing)
    zeroed = jnp.where(column == target, shaped, jnp.zeros((), source.dtype))
    return jnp.sum(zeroed, axis=1, dtype=source.dtype)


def put_rows(compact, wanted, stride, filler):
    trailing = (1,) * (compact.ndim - 2)
    target = wanted.reshape((1, 1, -1) + trailing)
    column = jnp.arange(stride, dtype=jnp.int32).reshape((1, stride, 1) + trailing)
    spread = jnp.where(column == target, compact[:, None], jnp.asarray(filler, compact.dtype))
    return spread.reshape((compact.shape[0] * stride,) + compact.shape[1:])


def exchange_order(count):
    bits = [1 << bit for bit in range(max(0, (count - 1).bit_length()))]
    order = []
    for first in range(0, len(bits), 2):
        order.extend(reversed(bits[first : first + 2]))
    return order


def spread(order, slots):
    table = np.zeros(slots, np.int32)
    for slot in range(slots):
        for bit, offset in enumerate(order):
            if slot >> bit & 1:
                table[slot] ^= offset
    return table


def extend(parts, spans, order):
    count = lax.axis_size("seq")
    live = sorted(range(len(parts)), key=lambda index: -spans[index])
    sizes = [part.shape[0] for part in parts]
    state = jnp.concatenate([parts[index] for index in live], axis=0)[None]
    finished = {}
    for offset in order + [None]:
        while live and spans[live[-1]] <= state.shape[0]:
            index = live.pop()
            start = sum(sizes[other] for other in live)
            finished[index] = state[:, start : start + sizes[index]]
            state = state[:, :start]
        if not live:
            break
        moved = lax.ppermute(state, "seq", [(source, source ^ offset) for source in range(count)])
        state = jnp.concatenate([state, moved], axis=0)
    return [finished[index] for index in range(len(parts))]


def split_exact(value):
    high = lax.reduce_precision(value, exponent_bits=8, mantissa_bits=7)
    rest = value - high
    middle = lax.reduce_precision(rest, exponent_bits=8, mantissa_bits=7)
    low = rest - middle
    return jnp.stack([high, middle, low]).astype(jnp.bfloat16)


def stats_rows(rows, heads_dev):
    return -(-(rows * heads_dev * 6) // (16 * lane)) * 16


def pack_stats(lse_sel, delta_sel):
    rows, heads_dev = lse_sel.shape
    coded = split_exact(jnp.stack([lse_sel.T, delta_sel.T])).reshape(-1)
    padded = stats_rows(rows, heads_dev) * lane
    coded = jnp.pad(coded, (0, padded - coded.shape[0]))
    return coded.reshape(padded // lane, lane)


def unpack_stats(coded, slots, rows, heads_dev):
    width = 2 * heads_dev * rows
    parts = coded.reshape(slots, -1)[:, : 3 * width].reshape(slots, 3, width)
    parts = parts.astype(jnp.float32)
    values = (parts[:, 0] + parts[:, 1]) + parts[:, 2]
    values = values.reshape(slots, 2, heads_dev, rows).transpose(1, 2, 0, 3)
    values = values.reshape(2, heads_dev, slots * rows)
    return values[0], values[1]


def shards(query_rows, key_rows, value_rows, cotangent, norm_gain, offsets):
    tok_dev, heads_dev, head_size = query_rows.shape
    seq_count = lax.axis_size("seq")
    device = lax.axis_index("seq")
    group_rows = tok_dev * seq_count // RATE4
    score_scale = head_size ** (-0.5)
    features = heads_dev * head_size * lax.axis_size("head")

    levels = []
    for stride in RATES:
        span = max(1, stride * group_rows // tok_dev)
        rows = tok_dev // stride
        wanted = offsets % stride
        levels.append(
            dict(
                stride=stride,
                span=span,
                rows=rows,
                wanted=wanted,
                spot=device % span,
                key_sel=pick_rows(key_rows, wanted, stride),
                value_sel=pick_rows(value_rows, wanted, stride),
                query_sel=pick_rows(query_rows, wanted, stride),
            )
        )
    spans = [level["span"] for level in levels]
    order = exchange_order(seq_count)
    for level in levels:
        level["owner"] = level["spot"] ^ jnp.asarray(spread(order, level["span"]))

    key_sets = extend(
        [
            jnp.concatenate(
                [
                    level["key_sel"].reshape(-1, lane),
                    level["value_sel"].reshape(-1, lane),
                    level["query_sel"].reshape(-1, lane),
                ],
                axis=0,
            )
            for level in levels
        ],
        spans,
        order,
    )

    lse_total = jnp.full((tok_dev, heads_dev), neg_fill, jnp.float32)
    for level, key_set in zip(levels, key_sets):
        span, rows = level["span"], level["rows"]
        paired = key_set.reshape(span, 3, rows, heads_dev, head_size)
        keys = paired[:, 0].reshape(span * rows, heads_dev, head_size)
        level["key_all"] = keys
        level["value_all"] = paired[:, 1].reshape(span * rows, heads_dev, head_size)
        level["query_all"] = paired[:, 2].reshape(span * rows, heads_dev, head_size)
        raw = (
            jnp.einsum("qhd,khd->hqk", level["query_sel"], keys, preferred_element_type=jnp.float32)
            * score_scale
        )
        key_at = (
            level["owner"][:, None] * rows + jnp.arange(rows, dtype=jnp.int32)[None, :]
        ).reshape(1, span * rows)
        query_at = (level["spot"] * rows + jnp.arange(rows, dtype=jnp.int32))[:, None]
        linked = key_at <= query_at
        scores = jnp.where(linked[None], raw, neg_fill)
        row_peak = jnp.max(scores, axis=2)
        level_lse = row_peak + jnp.log(jnp.sum(jnp.exp(scores - row_peak[:, :, None]), axis=2))
        level["scores"] = scores
        lse_total = jnp.logaddexp(
            lse_total, put_rows(level_lse.T, level["wanted"], level["stride"], neg_fill)
        )

    attended = jnp.zeros((tok_dev, heads_dev, head_size), jnp.float32)
    for level in levels:
        lse_sel = pick_rows(lse_total, level["wanted"], level["stride"])
        weights = jnp.exp(level["scores"] - lse_sel.T[:, :, None])
        level["lse_sel"] = lse_sel
        level["weights"] = weights
        out_sel = jnp.einsum(
            "hqk,khd->qhd", weights.astype(jnp.bfloat16), level["value_all"],
            preferred_element_type=jnp.float32,
        )
        attended = attended + put_rows(out_sel, level["wanted"], level["stride"], 0.0)

    grad_in = cotangent.astype(jnp.float32) * norm_gain[None]
    sums = lax.psum(
        jnp.stack(
            [
                jnp.sum(attended, axis=(1, 2)),
                jnp.sum(attended * attended, axis=(1, 2)),
                jnp.sum(grad_in, axis=(1, 2)),
                jnp.sum(grad_in * attended, axis=(1, 2)),
            ]
        ),
        "head",
    )
    centre = sums[0] / features
    variance = sums[1] / features - centre * centre
    inverse = lax.rsqrt(variance + epsilon)
    first_mean = sums[2] / features
    second_mean = inverse * (sums[3] / features - centre * first_mean)
    normed = (attended - centre[:, None, None]) * inverse[:, None, None]
    d_attended = (
        inverse[:, None, None]
        * (grad_in - first_mean[:, None, None] - normed * second_mean[:, None, None])
    ).astype(jnp.bfloat16)
    row_delta = jnp.sum(d_attended.astype(jnp.float32) * attended, axis=2)

    query_grad = jnp.zeros((tok_dev, heads_dev, head_size), jnp.float32)
    back_sets = []
    for level in levels:
        dout_sel = pick_rows(d_attended, level["wanted"], level["stride"])
        delta_sel = pick_rows(row_delta, level["wanted"], level["stride"])
        back_sets.append(
            jnp.concatenate(
                [dout_sel.reshape(-1, lane), pack_stats(level["lse_sel"], delta_sel)], axis=0
            )
        )
        weight_grad = jnp.einsum(
            "qhd,khd->hqk", dout_sel, level["value_all"], preferred_element_type=jnp.float32
        )
        score_grad = (level["weights"] * (weight_grad - delta_sel.T[:, :, None])).astype(
            jnp.bfloat16
        )
        grad_sel = jnp.einsum(
            "hqk,khd->qhd", score_grad, level["key_all"], preferred_element_type=jnp.float32
        )
        query_grad = query_grad + put_rows(
            grad_sel * score_scale, level["wanted"], level["stride"], 0.0
        )
    back_sets = extend(back_sets, spans, order)

    key_grad = jnp.zeros((tok_dev, heads_dev, head_size), jnp.float32)
    value_grad = jnp.zeros((tok_dev, heads_dev, head_size), jnp.float32)
    for level, back_set in zip(levels, back_sets):
        span, rows = level["span"], level["rows"]
        queries = level["query_all"]
        back_slots = back_set.reshape(span, -1, lane)
        dout_all = back_slots[:, : rows * heads_dev].reshape(span * rows, heads_dev, head_size)
        lse_all, delta_all = unpack_stats(
            back_slots[:, rows * heads_dev :], span, rows, heads_dev
        )
        raw = (
            jnp.einsum(
                "qhd,khd->hqk", queries, level["key_sel"], preferred_element_type=jnp.float32
            )
            * score_scale
        )
        query_at = (
            level["owner"][:, None] * rows + jnp.arange(rows, dtype=jnp.int32)[None, :]
        ).reshape(span * rows, 1)
        key_at = (level["spot"] * rows + jnp.arange(rows, dtype=jnp.int32))[None, :]
        linked = query_at >= key_at
        scores = jnp.where(linked[None], raw, neg_fill)
        weights = jnp.exp(scores - lse_all[:, :, None])
        value_grad_sel = jnp.einsum(
            "hqk,qhd->khd", weights.astype(jnp.bfloat16), dout_all,
            preferred_element_type=jnp.float32,
        )
        weight_grad = jnp.einsum(
            "qhd,khd->hqk", dout_all, level["value_sel"], preferred_element_type=jnp.float32
        )
        score_grad = (weights * (weight_grad - delta_all[:, :, None])).astype(jnp.bfloat16)
        key_grad_sel = jnp.einsum(
            "hqk,qhd->khd", score_grad, queries, preferred_element_type=jnp.float32
        )
        key_grad = key_grad + put_rows(
            key_grad_sel * score_scale, level["wanted"], level["stride"], 0.0
        )
        value_grad = value_grad + put_rows(value_grad_sel, level["wanted"], level["stride"], 0.0)

    return (
        query_grad.astype(jnp.bfloat16),
        key_grad.astype(jnp.bfloat16),
        value_grad.astype(jnp.bfloat16),
    )


def solution(mesh):
    placed = (
        P("seq", "head", None),
        P("seq", "head", None),
        P("seq", "head", None),
        P("seq", "head", None),
        P("head", None),
        P("head"),
    )
    return jax.shard_map(
        shards,
        mesh=mesh,
        in_specs=placed,
        out_specs=(P("seq", "head", None), P("seq", "head", None), P("seq", "head", None)),
        check_vma=False,
    )
```

```python
import numpy as np
import jax
import jax.numpy as jnp
from jax import lax
from jax.sharding import PartitionSpec as P

RATE2 = 4
RATE3 = 16
RATE4 = 32
RATES = (1, RATE2, RATE3, RATE4)

neg_fill = -1e30
epsilon = 1e-05
lane = 128


def pick_rows(source, wanted, stride):
    row_count = source.shape[0] // stride
    shaped = source.reshape((row_count, stride) + source.shape[1:])
    trailing = (1,) * (source.ndim - 2)
    target = wanted.reshape((1, 1, -1) + trailing)
    column = jnp.arange(stride, dtype=jnp.int32).reshape((1, stride, 1) + trailing)
    zeroed = jnp.where(column == target, shaped, jnp.zeros((), source.dtype))
    return jnp.sum(zeroed, axis=1, dtype=source.dtype)


def put_rows(compact, wanted, stride, filler):
    trailing = (1,) * (compact.ndim - 2)
    target = wanted.reshape((1, 1, -1) + trailing)
    column = jnp.arange(stride, dtype=jnp.int32).reshape((1, stride, 1) + trailing)
    spread = jnp.where(column == target, compact[:, None], jnp.asarray(filler, compact.dtype))
    return spread.reshape((compact.shape[0] * stride,) + compact.shape[1:])


def exchange_order(count):
    bits = [1 << bit for bit in range(max(0, (count - 1).bit_length()))]
    order = []
    for first in range(0, len(bits), 2):
        order.extend(reversed(bits[first : first + 2]))
    return order


def spread(order, slots):
    table = np.zeros(slots, np.int32)
    for slot in range(slots):
        for bit, offset in enumerate(order):
            if slot >> bit & 1:
                table[slot] ^= offset
    return table


def extend(parts, spans, order, toward):
    count = lax.axis_size("seq")
    live = sorted(range(len(parts)), key=lambda index: -spans[index])
    sizes = [part.shape[0] for part in parts]
    state = jnp.concatenate([parts[index] for index in live], axis=0)[None]
    finished = {}
    for offset in order + [None]:
        while live and spans[live[-1]] <= state.shape[0]:
            index = live.pop()
            start = sum(sizes[other] for other in live)
            finished[index] = state[:, start : start + sizes[index]]
            state = state[:, :start]
        if not live:
            break
        pairs = [(source, source ^ offset) for source in range(count)]
        if all(spans[index] <= 2 * state.shape[0] for index in live):
            pairs = [pair for pair in pairs if (pair[1] > pair[0]) == (toward > 0)]
        moved = lax.ppermute(state, "seq", pairs)
        state = jnp.concatenate([state, moved], axis=0)
    return [finished[index] for index in range(len(parts))]


def split_exact(value):
    high = lax.reduce_precision(value, exponent_bits=8, mantissa_bits=7)
    rest = value - high
    middle = lax.reduce_precision(rest, exponent_bits=8, mantissa_bits=7)
    low = rest - middle
    return jnp.stack([high, middle, low]).astype(jnp.bfloat16)


def stats_rows(rows, heads_dev):
    return -(-(rows * heads_dev * 6) // (16 * lane)) * 16


def pack_stats(lse_sel, delta_sel):
    rows, heads_dev = lse_sel.shape
    coded = split_exact(jnp.stack([lse_sel.T, delta_sel.T])).reshape(-1)
    padded = stats_rows(rows, heads_dev) * lane
    coded = jnp.pad(coded, (0, padded - coded.shape[0]))
    return coded.reshape(padded // lane, lane)


def unpack_stats(coded, slots, rows, heads_dev):
    width = 2 * heads_dev * rows
    parts = coded.reshape(slots, -1)[:, : 3 * width].reshape(slots, 3, width)
    parts = parts.astype(jnp.float32)
    values = (parts[:, 0] + parts[:, 1]) + parts[:, 2]
    values = values.reshape(slots, 2, heads_dev, rows).transpose(1, 2, 0, 3)
    values = values.reshape(2, heads_dev, slots * rows)
    return values[0], values[1]


def shards(query_rows, key_rows, value_rows, cotangent, norm_gain, offsets):
    tok_dev, heads_dev, head_size = query_rows.shape
    seq_count = lax.axis_size("seq")
    device = lax.axis_index("seq")
    group_rows = tok_dev * seq_count // RATE4
    score_scale = head_size ** (-0.5)
    features = heads_dev * head_size * lax.axis_size("head")

    levels = []
    for stride in RATES:
        span = max(1, stride * group_rows // tok_dev)
        rows = tok_dev // stride
        wanted = offsets % stride
        levels.append(
            dict(
                stride=stride,
                span=span,
                rows=rows,
                wanted=wanted,
                spot=device % span,
                key_sel=pick_rows(key_rows, wanted, stride),
                value_sel=pick_rows(value_rows, wanted, stride),
                query_sel=pick_rows(query_rows, wanted, stride),
            )
        )
    spans = [level["span"] for level in levels]
    order = exchange_order(seq_count)
    for level in levels:
        level["owner"] = level["spot"] ^ jnp.asarray(spread(order, level["span"]))

    key_sets = extend(
        [
            jnp.concatenate(
                [
                    level["key_sel"].reshape(-1, lane),
                    level["value_sel"].reshape(-1, lane),
                ],
                axis=0,
            )
            for level in levels
        ],
        spans,
        order,
        1,
    )
    query_sets = extend(
        [level["query_sel"].reshape(-1, lane) for level in levels], spans, order, -1
    )

    lse_total = jnp.full((tok_dev, heads_dev), neg_fill, jnp.float32)
    for level, key_set in zip(levels, key_sets):
        span, rows = level["span"], level["rows"]
        paired = key_set.reshape(span, 2, rows, heads_dev, head_size)
        keys = paired[:, 0].reshape(span * rows, heads_dev, head_size)
        level["key_all"] = keys
        level["value_all"] = paired[:, 1].reshape(span * rows, heads_dev, head_size)
        raw = (
            jnp.einsum("qhd,khd->hqk", level["query_sel"], keys, preferred_element_type=jnp.float32)
            * score_scale
        )
        key_at = (
            level["owner"][:, None] * rows + jnp.arange(rows, dtype=jnp.int32)[None, :]
        ).reshape(1, span * rows)
        query_at = (level["spot"] * rows + jnp.arange(rows, dtype=jnp.int32))[:, None]
        linked = key_at <= query_at
        scores = jnp.where(linked[None], raw, neg_fill)
        row_peak = jnp.max(scores, axis=2)
        level_lse = row_peak + jnp.log(jnp.sum(jnp.exp(scores - row_peak[:, :, None]), axis=2))
        level["scores"] = scores
        lse_total = jnp.logaddexp(
            lse_total, put_rows(level_lse.T, level["wanted"], level["stride"], neg_fill)
        )

    attended = jnp.zeros((tok_dev, heads_dev, head_size), jnp.float32)
    for level in levels:
        lse_sel = pick_rows(lse_total, level["wanted"], level["stride"])
        weights = jnp.exp(level["scores"] - lse_sel.T[:, :, None])
        level["lse_sel"] = lse_sel
        level["weights"] = weights
        out_sel = jnp.einsum(
            "hqk,khd->qhd", weights.astype(jnp.bfloat16), level["value_all"],
            preferred_element_type=jnp.float32,
        )
        attended = attended + put_rows(out_sel, level["wanted"], level["stride"], 0.0)

    grad_in = cotangent.astype(jnp.float32) * norm_gain[None]
    sums = lax.psum(
        jnp.stack(
            [
                jnp.sum(attended, axis=(1, 2)),
                jnp.sum(attended * attended, axis=(1, 2)),
                jnp.sum(grad_in, axis=(1, 2)),
                jnp.sum(grad_in * attended, axis=(1, 2)),
            ]
        ),
        "head",
    )
    centre = sums[0] / features
    variance = sums[1] / features - centre * centre
    inverse = lax.rsqrt(variance + epsilon)
    first_mean = sums[2] / features
    second_mean = inverse * (sums[3] / features - centre * first_mean)
    normed = (attended - centre[:, None, None]) * inverse[:, None, None]
    d_attended = (
        inverse[:, None, None]
        * (grad_in - first_mean[:, None, None] - normed * second_mean[:, None, None])
    ).astype(jnp.bfloat16)
    row_delta = jnp.sum(d_attended.astype(jnp.float32) * attended, axis=2)

    query_grad = jnp.zeros((tok_dev, heads_dev, head_size), jnp.float32)
    back_sets = []
    for level in levels:
        dout_sel = pick_rows(d_attended, level["wanted"], level["stride"])
        delta_sel = pick_rows(row_delta, level["wanted"], level["stride"])
        back_sets.append(
            jnp.concatenate(
                [dout_sel.reshape(-1, lane), pack_stats(level["lse_sel"], delta_sel)], axis=0
            )
        )
        weight_grad = jnp.einsum(
            "qhd,khd->hqk", dout_sel, level["value_all"], preferred_element_type=jnp.float32
        )
        score_grad = (level["weights"] * (weight_grad - delta_sel.T[:, :, None])).astype(
            jnp.bfloat16
        )
        grad_sel = jnp.einsum(
            "hqk,khd->qhd", score_grad, level["key_all"], preferred_element_type=jnp.float32
        )
        query_grad = query_grad + put_rows(
            grad_sel * score_scale, level["wanted"], level["stride"], 0.0
        )
    back_sets = extend(back_sets, spans, order, -1)

    key_grad = jnp.zeros((tok_dev, heads_dev, head_size), jnp.float32)
    value_grad = jnp.zeros((tok_dev, heads_dev, head_size), jnp.float32)
    for level, query_set, back_set in zip(levels, query_sets, back_sets):
        span, rows = level["span"], level["rows"]
        queries = query_set.reshape(span * rows, heads_dev, head_size)
        back_slots = back_set.reshape(span, -1, lane)
        dout_all = back_slots[:, : rows * heads_dev].reshape(span * rows, heads_dev, head_size)
        lse_all, delta_all = unpack_stats(
            back_slots[:, rows * heads_dev :], span, rows, heads_dev
        )
        raw = (
            jnp.einsum(
                "qhd,khd->hqk", queries, level["key_sel"], preferred_element_type=jnp.float32
            )
            * score_scale
        )
        query_at = (
            level["owner"][:, None] * rows + jnp.arange(rows, dtype=jnp.int32)[None, :]
        ).reshape(span * rows, 1)
        key_at = (level["spot"] * rows + jnp.arange(rows, dtype=jnp.int32))[None, :]
        linked = query_at >= key_at
        scores = jnp.where(linked[None], raw, neg_fill)
        weights = jnp.exp(scores - lse_all[:, :, None])
        value_grad_sel = jnp.einsum(
            "hqk,qhd->khd", weights.astype(jnp.bfloat16), dout_all,
            preferred_element_type=jnp.float32,
        )
        weight_grad = jnp.einsum(
            "qhd,khd->hqk", dout_all, level["value_sel"], preferred_element_type=jnp.float32
        )
        score_grad = (weights * (weight_grad - delta_all[:, :, None])).astype(jnp.bfloat16)
        key_grad_sel = jnp.einsum(
            "hqk,qhd->khd", score_grad, queries, preferred_element_type=jnp.float32
        )
        key_grad = key_grad + put_rows(
            key_grad_sel * score_scale, level["wanted"], level["stride"], 0.0
        )
        value_grad = value_grad + put_rows(value_grad_sel, level["wanted"], level["stride"], 0.0)

    return (
        query_grad.astype(jnp.bfloat16),
        key_grad.astype(jnp.bfloat16),
        value_grad.astype(jnp.bfloat16),
    )


def solution(mesh):
    placed = (
        P("seq", "head", None),
        P("seq", "head", None),
        P("seq", "head", None),
        P("seq", "head", None),
        P("head", None),
        P("head"),
    )
    return jax.shard_map(
        shards,
        mesh=mesh,
        in_specs=placed,
        out_specs=(P("seq", "head", None), P("seq", "head", None), P("seq", "head", None)),
        check_vma=False,
    )
```
